32 devices in a mesh: parts: 2 (over y), tm: 4 (over z), chan: 2 (over x), sub: 2 (over core).
Axes of the slice: x: 2, y: 2, z: 4, core: 2. Of those that a mesh axis runs over, the one named last changes fastest.
Arguments:
- start_state: float32 [16, 2048], P(('parts', 'chan')), parts along dimension 0, may hold values from -6 to 6
- guess: bfloat16 [64, 8, 2048], P(('parts', 'tm', 'sub'), 'chan'), parts along dimension 0, may hold values from -6 to 6
- w_in: bfloat16 [576, 320], replicated, may hold values from -0.25 to 0.25
- w_mid: bfloat16 [2880, 320], replicated, may hold values from -0.109375 to 0.109375
- w_out: bfloat16 [2880, 64], replicated, may hold values from -0.875 to 0.875
- time_embed: bfloat16 [1000, 320], replicated, may hold values from -4 to 4
- levels: float32 [1000], replicated, may hold values from 0 to 70, as said below
- plan: int32 [130], P('parts'), parts along dimension 0, may hold values from 0 to 999, as said below
- offset: int32 [2], P('parts'), parts along dimension 0, may hold values from 0 to 32
Outputs:
- trajectory: float32 [64, 8, 2048], P(('parts', 'tm', 'sub'), 'chan'), parts along dimension 0
The draws below stay inside these ranges and needn't reach their ends.
There are 2 independent parts, one for each index of `parts`. The reference program is written for one: setup_inputs(seed, part) draws one part's arguments, and reference() takes and returns one part's arrays. A program takes and returns all parts, laid end to end along the dimension named above; an argument that names none is the same for every part. Nothing has to cross between parts.
Inputs may be any that keep to these rules, and one draw needn't show every extreme that they name: `levels`: rises strictly with the timestep, by at most 0.07 from one timestep to the next. Strictly falling along the plan; the first entry is 999 and the last is 0.
All inputs are finite; a program needn't handle non-finite values.
Results may differ from the reference program's by a relative error of at most 0.003.
Values may be sent and summed in bfloat16 or wider, within the bound.
No kernel may reach another device: no remote copies, remote signals or barrier semaphores. Data moves between devices by JAX's collectives and lax.ppermute only.
A program may use at most 64 MiB of HBM per device.

```python
import jax
import jax.numpy as jnp
from jax import lax

C = 64
HID = 320
WT = 32
NT = 1000
ITERS = 2
H = 8
W = 32
SCHED = 64


def draw_levels(key, part):
    rises = jax.random.uniform(key, (NT,), jnp.float32, 0.02, 0.07)
    return jnp.cumsum(rises)


def draw_plan(key, part):
    inner = jax.random.permutation(key, NT - 2)[:SCHED - 1].astype(jnp.int32) + 1
    ends = jnp.array([0, NT - 1], dtype=jnp.int32)
    picked = jnp.concatenate([inner, ends])
    return (-jnp.sort(-picked)).astype(jnp.int32)


def level_of(key, shape, cuts, smallest, high):
    def one(position, parts):
        steps = jax.random.uniform(jax.random.fold_in(jax.random.fold_in(key, 6), position), (parts,), jnp.float32, smallest / len(cuts), high / len(cuts))
        return jnp.repeat(jnp.exp(steps), shape[position] // parts).reshape((-1,) + (1,) * (len(shape) - position - 1))

    factor_of = one(*cuts[0])
    for cut in cuts[1:]:
        factor_of = factor_of * one(*cut)
    return factor_of


def normal_values(stream_key, extent, deviation, limit, split=(), kind=jnp.bfloat16):
    values = deviation * jax.random.normal(stream_key, extent, jnp.float32)
    if split:
        values = values * level_of(stream_key, extent, split, -0.22, 0.18)
    return jnp.clip(values, -limit, limit).astype(kind)


def setup_inputs(seed: int = 0, part: int = 0) -> dict:
    key_of = jax.random.split(jax.random.key(seed), 10)
    part_splits = jax.random.split(jax.random.fold_in(key_of[9], part), 10)
    return {
        "start_state": normal_values(part_splits[0], (H, WT * C), 1.0, 6.0, ((0, 2),), jnp.float32),
        "guess": normal_values(part_splits[1], (W, H, WT * C), 1.0, 6.0, ((0, 8), (1, 2))),
        "w_in": normal_values(key_of[2], (9 * C, HID), (9 * C) ** -0.5, 0.25),
        "w_mid": normal_values(key_of[3], (9 * HID, HID), (9 * HID) ** -0.5, 0.109375),
        "w_out": normal_values(key_of[4], (9 * HID, C), (9 * HID // 64) ** -0.5, 0.875),
        "time_embed": normal_values(key_of[5], (NT, HID), 1.0, 4.0),
        "levels": draw_levels(jax.random.fold_in(key_of[9], 71), part),
        "plan": draw_plan(jax.random.fold_in(jax.random.fold_in(key_of[9], part), 71), part),
        "offset": jax.random.randint(part_splits[8], (1,), 0, W + 1).astype(jnp.int32),
    }


def conv_same(layer_in, weight):
    channels = layer_in.shape[-1]
    kernel = weight.astype(jnp.float32).reshape(3, 3, channels, weight.shape[1])
    return lax.conv_general_dilated(layer_in, kernel, (1, 1), "SAME", dimension_numbers=("NHWC", "HWIO", "NHWC"), precision=lax.Precision.HIGHEST)


def drift_block(layer_in, embed, w_in, w_mid, w_out):
    block_steps, tile_rows, merged = layer_in.shape
    channels = w_out.shape[1]
    tiles = layer_in.astype(jnp.float32).reshape(block_steps, tile_rows, merged // channels, channels)
    first_hidden = jax.nn.silu(conv_same(tiles, w_in) + embed[:, None, None, :]).astype(jnp.bfloat16)
    first_hidden = lax.optimization_barrier(first_hidden).astype(jnp.float32)
    second_hidden = jax.nn.silu(conv_same(first_hidden, w_mid)).astype(jnp.bfloat16)
    second_hidden = lax.optimization_barrier(second_hidden).astype(jnp.float32)
    drift_out = conv_same(second_hidden, w_out)
    return drift_out.reshape(block_steps, tile_rows, merged)


def reference(start_state, guess, w_in, w_mid, w_out, time_embed, levels, plan, offset):
    window = guess.shape[0]
    window_ids = lax.dynamic_slice_in_dim(plan, offset[0].astype(jnp.int32), window + 1)
    noise = levels[window_ids]
    step_size = noise[1:] - noise[:-1]
    embed = time_embed[window_ids[:-1]].astype(jnp.float32)
    factor = jnp.where(jnp.arange(window) == 0, 1.0, 1.5).astype(jnp.float32)
    layer_in = guess
    states_after = None
    for sweep in range(ITERS):
        blocks = layer_in.reshape(window // 8, 8, guess.shape[1], guess.shape[2])
        embed_blocks = embed.reshape(window // 8, 8, embed.shape[1])
        drift_all = lax.map(lambda pair: drift_block(pair[0], pair[1], w_in, w_mid, w_out), (blocks, embed_blocks))
        drift_all = drift_all.reshape(guess.shape)
        earlier = jnp.concatenate([jnp.zeros_like(drift_all[:1]), drift_all[:-1]], axis=0)
        increment = step_size[:, None, None] * (factor[:, None, None] * drift_all - 0.5 * earlier)
        running = jnp.cumsum(increment, axis=0)
        states_after = start_state[None] + running
        states_before = states_after - increment
        layer_in = states_before.astype(jnp.bfloat16)
    return states_after
```

```python
import jax
import jax.numpy as jnp
from jax import lax
from jax.experimental import pallas as pl
from jax.experimental.pallas import tpu as pltpu
from jax.sharding import PartitionSpec as P

ITERS = 2
TIME_AXES = ("tm", "sub")


def padded_2(block, sides, width):
    for axis, dim in sides:
        count = lax.axis_size(axis)
        forward = [(i, i + 1) for i in range(count - 1)]
        backward = [(target, source) for source, target in forward]
        low = lax.ppermute(
            lax.slice_in_dim(block, block.shape[dim] - width, None, axis=dim), axis, forward
        )
        high = lax.ppermute(lax.slice_in_dim(block, 0, width, axis=dim), axis, backward)
        block = jnp.concatenate([low, block, high], axis=dim)
    return block


def conv3x3(src_ref, w_ref, rows_out):
    steps, _, columns, channels_in = src_ref.shape
    channels_out = w_ref.shape[-1]
    size = steps * rows_out * columns
    taps = []
    for col_off in range(3):
        acc = None
        for row_off in range(3):
            patch = src_ref[:, row_off : row_off + rows_out].reshape(size, channels_in)
            part = jnp.dot(patch, w_ref[row_off * 3 + col_off], preferred_element_type=jnp.float32)
            acc = part if acc is None else acc + part
        taps.append(acc)
    column = lax.broadcasted_iota(jnp.int32, (steps * rows_out, columns, channels_out), 1)
    column = column.reshape(size, channels_out)
    left = jnp.where(column == 0, 0.0, pltpu.roll(taps[0], 1, 0))
    right = jnp.where(column == columns - 1, 0.0, pltpu.roll(taps[2], size - 1, 0))
    return (left + taps[1] + right).reshape(steps, rows_out, columns, channels_out)


def silu(v):
    return v / (1.0 + jnp.exp(-v))


def row_valid(shape, first_row, total_rows):
    rows = first_row + lax.broadcasted_iota(jnp.int32, shape, 1)
    return (rows >= 0) & (rows < total_rows)


def drift_kernel(total_rows, first_ref, x_ref, emb_ref, w1_ref, w2_ref, w3_ref, out_ref, h1_ref, h2_ref):
    first_row = first_ref[0]
    steps, rows_1, columns, hidden = h1_ref.shape
    rows_2 = h2_ref.shape[1]
    act = conv3x3(x_ref, w1_ref, rows_1) + emb_ref[...][:, None, None, :]
    act = jnp.where(row_valid(act.shape, first_row, total_rows), silu(act), 0.0)
    h1_ref[...] = act.astype(jnp.bfloat16)
    act = conv3x3(h1_ref, w2_ref, rows_2)
    act = jnp.where(row_valid(act.shape, first_row + 1, total_rows), silu(act), 0.0)
    h2_ref[...] = act.astype(jnp.bfloat16)
    out_ref[...] = conv3x3(h2_ref, w3_ref, out_ref.shape[1])


def drift(layer_in, embed, w_in, w_mid, w_out):
    steps_dev, tile_rows, merged = layer_in.shape
    channels = w_out.shape[1]
    hidden = w_in.shape[1]
    columns = merged // channels
    rimmed = padded_2(layer_in, (("chan", 1),), 3)
    first_row = lax.axis_index("chan") * tile_rows - 2
    total_rows = tile_rows * lax.axis_size("chan")
    x = rimmed.reshape(steps_dev, tile_rows + 6, columns, channels)
    w1 = w_in.reshape(9, channels, hidden)
    w2 = w_mid.reshape(9, hidden, hidden)
    w3 = w_out.reshape(9, hidden, channels)
    rows = (tile_rows + 4) + (tile_rows + 2) + tile_rows
    flops = 2 * steps_dev * columns * 9 * hidden * (channels * (tile_rows + 4) + hidden * (tile_rows + 2) + channels * tile_rows)
    vmem = pl.BlockSpec(memory_space=pltpu.VMEM)
    out = pl.pallas_call(
        lambda *refs: drift_kernel(total_rows, *refs),
        out_shape=jax.ShapeDtypeStruct((steps_dev, tile_rows, columns, channels), jnp.float32),
        in_specs=[pl.BlockSpec(memory_space=pltpu.SMEM)] + [vmem] * 5,
        out_specs=vmem,
        scratch_shapes=[
            pltpu.VMEM((steps_dev, tile_rows + 4, columns, hidden), jnp.bfloat16),
            pltpu.VMEM((steps_dev, tile_rows + 2, columns, hidden), jnp.bfloat16),
        ],
        compiler_params=pltpu.CompilerParams(vmem_limit_bytes=48 * 1024 * 1024),
        cost_estimate=pl.CostEstimate(
            flops=flops,
            transcendentals=steps_dev * columns * hidden * rows,
            bytes_accessed=2 * (w1.size + w2.size + w3.size) + 2 * x.size + 4 * steps_dev * tile_rows * merged,
        ),
    )(first_row.reshape(1).astype(jnp.int32), x, embed, w1, w2, w3)
    return out.reshape(steps_dev, tile_rows, merged)


def shifted(array, by):
    devices = lax.axis_size(TIME_AXES)
    pairs = [(i, i + by) for i in range(devices - by)]
    return lax.ppermute(array, TIME_AXES, pairs)


def scan_earlier(total, carried):
    devices = lax.axis_size(TIME_AXES)
    if carried is None:
        got = shifted(total, 1)
        moved = None
    else:
        both = shifted(jnp.stack([total, carried]), 1)
        got, moved = both[0], both[1]
    earlier = got
    running = total + got
    by = 2
    while by < devices:
        got = shifted(running, by)
        earlier = earlier + got
        if by * 2 < devices:
            running = running + got
        by *= 2
    return earlier, moved


def shards(start_state, guess, w_in, w_mid, w_out, time_embed, levels, plan, offset):
    steps_dev = guess.shape[0]
    devices = lax.axis_size(TIME_AXES)
    time_index = lax.axis_index(TIME_AXES)
    first_step = time_index * steps_dev
    window_ids = lax.dynamic_slice_in_dim(plan, offset[0] + first_step, steps_dev + 1)
    after_id = lax.dynamic_slice_in_dim(
        plan, jnp.minimum(offset[0] + first_step + steps_dev + 1, plan.shape[0] - 1), 1
    )
    all_ids = jnp.concatenate([window_ids, after_id])
    one_hot = all_ids[:, None] == jnp.arange(levels.shape[0], dtype=jnp.int32)[None, :]
    noise = jnp.dot(one_hot.astype(jnp.float32), levels, precision=lax.Precision.HIGHEST)
    step_size = noise[1 : steps_dev + 1] - noise[:steps_dev]
    next_step = jnp.where(time_index < devices - 1, noise[steps_dev + 1] - noise[steps_dev], 0.0)
    embed = jnp.dot(
        one_hot[:steps_dev].astype(jnp.bfloat16), time_embed, preferred_element_type=jnp.float32
    )
    factor = jnp.where(first_step + jnp.arange(steps_dev, dtype=jnp.int32) == 0, 1.0, 1.5).astype(
        jnp.float32
    )
    layer_in = guess
    states_after = None
    for sweep in range(ITERS):
        last_sweep = sweep == ITERS - 1
        drift_now = drift(layer_in, embed, w_in, w_mid, w_out)
        earlier_local = jnp.concatenate([jnp.zeros_like(drift_now[:1]), drift_now[:-1]], axis=0)
        increment = step_size[:, None, None] * (factor[:, None, None] * drift_now - 0.5 * earlier_local)
        running = jnp.cumsum(increment, axis=0)
        handed_on = running[-1] - 0.5 * next_step * drift_now[-1]
        earlier_sum, previous = scan_earlier(handed_on, None if last_sweep else drift_now[-1])
        states_after = (start_state + earlier_sum)[None] + running
        if not last_sweep:
            first_extra = -0.5 * step_size[0] * previous
            states_before = states_after - increment
            states_before = states_before.at[0].add(-first_extra)
            layer_in = states_before.astype(jnp.bfloat16)
    return states_after


def solution(mesh):
    return jax.shard_map(
        shards,
        mesh=mesh,
        in_specs=(
            P(("parts", "chan"), None),
            P(("parts", "tm", "sub"), "chan", None),
            P(),
            P(),
            P(),
            P(),
            P(),
            P("parts"),
            P("parts"),
        ),
        out_specs=P(("parts", "tm", "sub"), "chan", None),
        check_vma=False,
    )
```

```python
import jax
import jax.numpy as jnp
from jax import lax
from jax.experimental import pallas as pl
from jax.experimental.pallas import tpu as pltpu
from jax.sharding import PartitionSpec as P

ITERS = 2
TIME_AXES = ("tm", "sub")


def padded_2(block, sides, width):
    for axis, dim in sides:
        count = lax.axis_size(axis)
        forward = [(i, i + 1) for i in range(count - 1)]
        backward = [(target, source) for source, target in forward]
        low = lax.ppermute(
            lax.slice_in_dim(block, block.shape[dim] - width, None, axis=dim), axis, forward
        )
        high = lax.ppermute(lax.slice_in_dim(block, 0, width, axis=dim), axis, backward)
        block = jnp.concatenate([low, block, high], axis=dim)
    return block


def conv3x3(src_ref, w_ref, rows_out):
    steps, _, columns, channels_in = src_ref.shape
    channels_out = w_ref.shape[-1]
    size = steps * rows_out * columns
    taps = []
    for col_off in range(3):
        acc = None
        for row_off in range(3):
            patch = src_ref[:, row_off : row_off + rows_out].reshape(size, channels_in)
            part = jnp.dot(patch, w_ref[row_off * 3 + col_off], preferred_element_type=jnp.float32)
            acc = part if acc is None else acc + part
        taps.append(acc)
    column = lax.broadcasted_iota(jnp.int32, (steps * rows_out, columns, channels_out), 1)
    column = column.reshape(size, channels_out)
    left = jnp.where(column == 0, 0.0, pltpu.roll(taps[0], 1, 0))
    right = jnp.where(column == columns - 1, 0.0, pltpu.roll(taps[2], size - 1, 0))
    return (left + taps[1] + right).reshape(steps, rows_out, columns, channels_out)


def silu(v):
    return v / (1.0 + jnp.exp(-v))


def row_valid(shape, first_row, total_rows):
    rows = first_row + lax.broadcasted_iota(jnp.int32, shape, 1)
    return (rows >= 0) & (rows < total_rows)


def drift_kernel(total_rows, first_ref, x_ref, emb_ref, w1_ref, w2_ref, w3_ref, out_ref, h1_ref, h2_ref):
    first_row = first_ref[0]
    steps, rows_1, columns, hidden = h1_ref.shape
    rows_2 = h2_ref.shape[1]
    act = conv3x3(x_ref, w1_ref, rows_1) + emb_ref[...][:, None, None, :]
    act = jnp.where(row_valid(act.shape, first_row, total_rows), silu(act), 0.0)
    h1_ref[...] = act.astype(jnp.bfloat16)
    act = conv3x3(h1_ref, w2_ref, rows_2)
    act = jnp.where(row_valid(act.shape, first_row + 1, total_rows), silu(act), 0.0)
    h2_ref[...] = act.astype(jnp.bfloat16)
    out_ref[...] = conv3x3(h2_ref, w3_ref, out_ref.shape[1])


def drift(layer_in, embed, w_in, w_mid, w_out):
    steps_dev, tile_rows, merged = layer_in.shape
    channels = w_out.shape[1]
    hidden = w_in.shape[1]
    columns = merged // channels
    rimmed = padded_2(layer_in, (("chan", 1),), 3)
    first_row = lax.axis_index("chan") * tile_rows - 2
    total_rows = tile_rows * lax.axis_size("chan")
    x = rimmed.reshape(steps_dev, tile_rows + 6, columns, channels)
    w1 = w_in.reshape(9, channels, hidden)
    w2 = w_mid.reshape(9, hidden, hidden)
    w3 = w_out.reshape(9, hidden, channels)
    rows = (tile_rows + 4) + (tile_rows + 2) + tile_rows
    flops = 2 * steps_dev * columns * 9 * hidden * (channels * (tile_rows + 4) + hidden * (tile_rows + 2) + channels * tile_rows)
    vmem = pl.BlockSpec(memory_space=pltpu.VMEM)
    out = pl.pallas_call(
        lambda *refs: drift_kernel(total_rows, *refs),
        out_shape=jax.ShapeDtypeStruct((steps_dev, tile_rows, columns, channels), jnp.float32),
        in_specs=[pl.BlockSpec(memory_space=pltpu.SMEM)] + [vmem] * 5,
        out_specs=vmem,
        scratch_shapes=[
            pltpu.VMEM((steps_dev, tile_rows + 4, columns, hidden), jnp.bfloat16),
            pltpu.VMEM((steps_dev, tile_rows + 2, columns, hidden), jnp.bfloat16),
        ],
        compiler_params=pltpu.CompilerParams(vmem_limit_bytes=48 * 1024 * 1024),
        cost_estimate=pl.CostEstimate(
            flops=flops,
            transcendentals=steps_dev * columns * hidden * rows,
            bytes_accessed=2 * (w1.size + w2.size + w3.size) + 2 * x.size + 4 * steps_dev * tile_rows * merged,
        ),
    )(first_row.reshape(1).astype(jnp.int32), x, embed, w1, w2, w3)
    return out.reshape(steps_dev, tile_rows, merged)


def shifted(array, by):
    devices = lax.axis_size(TIME_AXES)
    pairs = [(i, i + by) for i in range(devices - by)]
    return lax.ppermute(array, TIME_AXES, pairs)


def scan_earlier(total, carried):
    devices = lax.axis_size(TIME_AXES)
    radix = min(devices, 8)
    earlier = None
    window = total
    moved = None
    stride = 1
    while stride < devices:
        got_all = []
        for k in range(1, radix):
            by = k * stride
            if by >= devices:
                break
            if by == 1 and carried is not None:
                both = shifted(jnp.stack([window, carried]), 1)
                got, moved = both[0], both[1]
            else:
                got = shifted(window, by)
            got_all.append(got)
        gathered = got_all[0]
        for got in got_all[1:]:
            gathered = gathered + got
        earlier = gathered if earlier is None else earlier + gathered
        stride *= radix
        if stride < devices:
            window = window + gathered
    return earlier, moved


def shards(start_state, guess, w_in, w_mid, w_out, time_embed, levels, plan, offset):
    steps_dev = guess.shape[0]
    devices = lax.axis_size(TIME_AXES)
    time_index = lax.axis_index(TIME_AXES)
    first_step = time_index * steps_dev
    window_ids = lax.dynamic_slice_in_dim(plan, offset[0] + first_step, steps_dev + 1)
    after_id = lax.dynamic_slice_in_dim(
        plan, jnp.minimum(offset[0] + first_step + steps_dev + 1, plan.shape[0] - 1), 1
    )
    all_ids = jnp.concatenate([window_ids, after_id])
    one_hot = all_ids[:, None] == jnp.arange(levels.shape[0], dtype=jnp.int32)[None, :]
    noise = jnp.dot(one_hot.astype(jnp.float32), levels, precision=lax.Precision.HIGHEST)
    step_size = noise[1 : steps_dev + 1] - noise[:steps_dev]
    next_step = jnp.where(time_index < devices - 1, noise[steps_dev + 1] - noise[steps_dev], 0.0)
    embed = jnp.dot(
        one_hot[:steps_dev].astype(jnp.bfloat16), time_embed, preferred_element_type=jnp.float32
    )
    factor = jnp.where(first_step + jnp.arange(steps_dev, dtype=jnp.int32) == 0, 1.0, 1.5).astype(
        jnp.float32
    )
    layer_in = guess
    states_after = None
    for sweep in range(ITERS):
        last_sweep = sweep == ITERS - 1
        drift_now = drift(layer_in, embed, w_in, w_mid, w_out)
        earlier_local = jnp.concatenate([jnp.zeros_like(drift_now[:1]), drift_now[:-1]], axis=0)
        increment = step_size[:, None, None] * (factor[:, None, None] * drift_now - 0.5 * earlier_local)
        running = jnp.cumsum(increment, axis=0)
        handed_on = running[-1] - 0.5 * next_step * drift_now[-1]
        earlier_sum, previous = scan_earlier(handed_on, None if last_sweep else drift_now[-1])
        states_after = (start_state + earlier_sum)[None] + running
        if not last_sweep:
            first_extra = -0.5 * step_size[0] * previous
            states_before = states_after - increment
            states_before = states_before.at[0].add(-first_extra)
            layer_in = states_before.astype(jnp.bfloat16)
    return states_after


def solution(mesh):
    return jax.shard_map(
        shards,
        mesh=mesh,
        in_specs=(
            P(("parts", "chan"), None),
            P(("parts", "tm", "sub"), "chan", None),
            P(),
            P(),
            P(),
            P(),
            P(),
            P("parts"),
            P("parts"),
        ),
        out_specs=P(("parts", "tm", "sub"), "chan", None),
        check_vma=False,
    )
```

```python
import jax
import jax.numpy as jnp
from jax import lax
from jax.experimental import pallas as pl
from jax.experimental.pallas import tpu as pltpu
from jax.sharding import PartitionSpec as P

ITERS = 2
TIME_AXES = ("tm", "sub")


def padded_2(block, sides, width):
    for axis, dim in sides:
        count = lax.axis_size(axis)
        forward = [(i, i + 1) for i in range(count - 1)]
        backward = [(target, source) for source, target in forward]
        low = lax.ppermute(
            lax.slice_in_dim(block, block.shape[dim] - width, None, axis=dim), axis, forward
        )
        high = lax.ppermute(lax.slice_in_dim(block, 0, width, axis=dim), axis, backward)
        block = jnp.concatenate([low, block, high], axis=dim)
    return block


def conv3x3(src_ref, w_ref, rows_out):
    steps, _, columns, channels_in = src_ref.shape
    channels_out = w_ref.shape[0]
    size = steps * rows_out * columns
    taps = []
    for col_off in range(3):
        acc = None
        for row_off in range(3):
            patch = src_ref[:, row_off : row_off + rows_out].reshape(size, channels_in)
            tap = row_off * 3 + col_off
            weight = w_ref[:, tap * channels_in : (tap + 1) * channels_in]
            part = lax.dot_general(
                patch, weight, (((1,), (1,)), ((), ())), preferred_element_type=jnp.float32
            )
            acc = part if acc is None else acc + part
        taps.append(acc)
    column = lax.broadcasted_iota(jnp.int32, (steps * rows_out, columns, channels_out), 1)
    column = column.reshape(size, channels_out)
    left = jnp.where(column == 0, 0.0, pltpu.roll(taps[0], 1, 0))
    right = jnp.where(column == columns - 1, 0.0, pltpu.roll(taps[2], size - 1, 0))
    return (left + taps[1] + right).reshape(steps, rows_out, columns, channels_out)


def silu(v):
    return v / (1.0 + jnp.exp(-v))


def row_valid(shape, first_row, total_rows):
    rows = first_row + lax.broadcasted_iota(jnp.int32, shape, 1)
    return (rows >= 0) & (rows < total_rows)


def drift_kernel(total_rows, first_ref, x_ref, emb_ref, w1_ref, w2_ref, w3_ref, out_ref, h1_ref, h2_ref):
    first_row = first_ref[0]
    steps, rows_1, columns, hidden = h1_ref.shape
    rows_2 = h2_ref.shape[1]
    act = conv3x3(x_ref, w1_ref, rows_1) + emb_ref[...][:, None, None, :]
    act = jnp.where(row_valid(act.shape, first_row, total_rows), silu(act), 0.0)
    h1_ref[...] = act.astype(jnp.bfloat16)
    act = conv3x3(h1_ref, w2_ref, rows_2)
    act = jnp.where(row_valid(act.shape, first_row + 1, total_rows), silu(act), 0.0)
    h2_ref[...] = act.astype(jnp.bfloat16)
    out_ref[...] = conv3x3(h2_ref, w3_ref, out_ref.shape[1])


def drift(layer_in, embed, w_in, w_mid, w_out):
    steps_dev, tile_rows, merged = layer_in.shape
    channels = w_out.shape[1]
    hidden = w_in.shape[1]
    columns = merged // channels
    rimmed = padded_2(layer_in, (("chan", 1),), 3)
    first_row = lax.axis_index("chan") * tile_rows - 2
    total_rows = tile_rows * lax.axis_size("chan")
    x = rimmed.reshape(steps_dev, tile_rows + 6, columns, channels)
    w1, w2, w3 = w_in.T, w_mid.T, w_out.T
    rows = (tile_rows + 4) + (tile_rows + 2) + tile_rows
    flops = 2 * steps_dev * columns * 9 * hidden * (channels * (tile_rows + 4) + hidden * (tile_rows + 2) + channels * tile_rows)
    vmem = pl.BlockSpec(memory_space=pltpu.VMEM)
    out = pl.pallas_call(
        lambda *refs: drift_kernel(total_rows, *refs),
        out_shape=jax.ShapeDtypeStruct((steps_dev, tile_rows, columns, channels), jnp.float32),
        in_specs=[pl.BlockSpec(memory_space=pltpu.SMEM)] + [vmem] * 5,
        out_specs=vmem,
        scratch_shapes=[
            pltpu.VMEM((steps_dev, tile_rows + 4, columns, hidden), jnp.bfloat16),
            pltpu.VMEM((steps_dev, tile_rows + 2, columns, hidden), jnp.bfloat16),
        ],
        compiler_params=pltpu.CompilerParams(vmem_limit_bytes=48 * 1024 * 1024),
        cost_estimate=pl.CostEstimate(
            flops=flops,
            transcendentals=steps_dev * columns * hidden * rows,
            bytes_accessed=2 * (w1.size + w2.size + w3.size) + 2 * x.size + 4 * steps_dev * tile_rows * merged,
        ),
    )(first_row.reshape(1).astype(jnp.int32), x, embed, w1, w2, w3)
    return out.reshape(steps_dev, tile_rows, merged)


def shifted(array, by):
    devices = lax.axis_size(TIME_AXES)
    pairs = [(i, i + by) for i in range(devices - by)]
    return lax.ppermute(array, TIME_AXES, pairs)


def scan_earlier(total, carried):
    devices = lax.axis_size(TIME_AXES)
    radix = min(devices, 8)
    earlier = None
    window = total
    moved = None
    stride = 1
    while stride < devices:
        got_all = []
        for k in range(1, radix):
            by = k * stride
            if by >= devices:
                break
            if by == 1 and carried is not None:
                both = shifted(jnp.stack([window, carried]), 1)
                got, moved = both[0], both[1]
            else:
                got = shifted(window, by)
            got_all.append(got)
        gathered = got_all[0]
        for got in got_all[1:]:
            gathered = gathered + got
        earlier = gathered if earlier is None else earlier + gathered
        stride *= radix
        if stride < devices:
            window = window + gathered
    return earlier, moved


def shards(start_state, guess, w_in, w_mid, w_out, time_embed, levels, plan, offset):
    steps_dev = guess.shape[0]
    devices = lax.axis_size(TIME_AXES)
    time_index = lax.axis_index(TIME_AXES)
    first_step = time_index * steps_dev
    window_ids = lax.dynamic_slice_in_dim(plan, offset[0] + first_step, steps_dev + 1)
    after_id = lax.dynamic_slice_in_dim(
        plan, jnp.minimum(offset[0] + first_step + steps_dev + 1, plan.shape[0] - 1), 1
    )
    all_ids = jnp.concatenate([window_ids, after_id])
    one_hot = all_ids[:, None] == jnp.arange(levels.shape[0], dtype=jnp.int32)[None, :]
    noise = jnp.dot(one_hot.astype(jnp.float32), levels, precision=lax.Precision.HIGHEST)
    step_size = noise[1 : steps_dev + 1] - noise[:steps_dev]
    next_step = jnp.where(time_index < devices - 1, noise[steps_dev + 1] - noise[steps_dev], 0.0)
    embed = jnp.dot(
        one_hot[:steps_dev].astype(jnp.bfloat16), time_embed, preferred_element_type=jnp.float32
    )
    factor = jnp.where(first_step + jnp.arange(steps_dev, dtype=jnp.int32) == 0, 1.0, 1.5).astype(
        jnp.float32
    )
    layer_in = guess
    states_after = None
    for sweep in range(ITERS):
        last_sweep = sweep == ITERS - 1
        drift_now = drift(layer_in, embed, w_in, w_mid, w_out)
        earlier_local = jnp.concatenate([jnp.zeros_like(drift_now[:1]), drift_now[:-1]], axis=0)
        increment = step_size[:, None, None] * (factor[:, None, None] * drift_now - 0.5 * earlier_local)
        running = jnp.cumsum(increment, axis=0)
        handed_on = running[-1] - 0.5 * next_step * drift_now[-1]
        earlier_sum, previous = scan_earlier(handed_on, None if last_sweep else drift_now[-1])
        states_after = (start_state + earlier_sum)[None] + running
        if not last_sweep:
            first_extra = -0.5 * step_size[0] * previous
            states_before = states_after - increment
            states_before = states_before.at[0].add(-first_extra)
            layer_in = states_before.astype(jnp.bfloat16)
    return states_after


def solution(mesh):
    return jax.shard_map(
        shards,
        mesh=mesh,
        in_specs=(
            P(("parts", "chan"), None),
            P(("parts", "tm", "sub"), "chan", None),
            P(),
            P(),
            P(),
            P(),
            P(),
            P("parts"),
            P("parts"),
        ),
        out_specs=P(("parts", "tm", "sub"), "chan", None),
        check_vma=False,
    )
```

```python
import jax
import jax.numpy as jnp
from jax import lax
from jax.experimental import pallas as pl
from jax.experimental.pallas import tpu as pltpu
from jax.sharding import PartitionSpec as P

ITERS = 2
TIME_AXES = ("tm", "sub")


def padded_2(block, sides, width):
    for axis, dim in sides:
        count = lax.axis_size(axis)
        forward = [(i, i + 1) for i in range(count - 1)]
        backward = [(target, source) for source, target in forward]
        low = lax.ppermute(
            lax.slice_in_dim(block, block.shape[dim] - width, None, axis=dim), axis, forward
        )
        high = lax.ppermute(lax.slice_in_dim(block, 0, width, axis=dim), axis, backward)
        block = jnp.concatenate([low, block, high], axis=dim)
    return block


def conv3x3(src_ref, w_ref, rows_out):
    steps, _, columns, channels_in = src_ref.shape
    channels_out = w_ref.shape[0]
    size = steps * rows_out * columns
    taps = []
    for col_off in range(3):
        acc = None
        for row_off in range(3):
            patch = src_ref[:, row_off : row_off + rows_out].reshape(size, channels_in)
            tap = row_off * 3 + col_off
            weight = w_ref[:, tap * channels_in : (tap + 1) * channels_in]
            part = lax.dot_general(
                patch, weight, (((1,), (1,)), ((), ())), preferred_element_type=jnp.float32
            )
            acc = part if acc is None else acc + part
        taps.append(acc)
    column = lax.broadcasted_iota(jnp.int32, (steps * rows_out, columns, channels_out), 1)
    column = column.reshape(size, channels_out)
    left = jnp.where(column == 0, 0.0, pltpu.roll(taps[0], 1, 0))
    right = jnp.where(column == columns - 1, 0.0, pltpu.roll(taps[2], size - 1, 0))
    return (left + taps[1] + right).reshape(steps, rows_out, columns, channels_out)


def silu(v):
    return v / (1.0 + jnp.exp(-v))


def row_valid(shape, first_row, total_rows):
    rows = first_row + lax.broadcasted_iota(jnp.int32, shape, 1)
    return (rows >= 0) & (rows < total_rows)


def drift_kernel(total_rows, same, first_ref, x_ref, emb_ref, w1_ref, w2_ref, w3_ref, out_ref, h1_ref, h2_ref):
    first_row = first_ref[0]
    margin = 1 if same else 0
    rows_1 = h1_ref.shape[1] - 2 * margin
    rows_2 = h2_ref.shape[1] - 2 * margin
    act = conv3x3(x_ref, w1_ref, rows_1) + emb_ref[...][:, None, None, :]
    act = jnp.where(row_valid(act.shape, first_row, total_rows), silu(act), 0.0)
    store_hidden(h1_ref, act.astype(jnp.bfloat16), margin)
    act = conv3x3(h1_ref, w2_ref, rows_2)
    act = jnp.where(row_valid(act.shape, first_row + 1 - margin, total_rows), silu(act), 0.0)
    store_hidden(h2_ref, act.astype(jnp.bfloat16), margin)
    out_ref[...] = conv3x3(h2_ref, w3_ref, out_ref.shape[1])


def store_hidden(ref, value, margin):
    if margin:
        edge = jnp.zeros((ref.shape[0], margin) + ref.shape[2:], ref.dtype)
        ref[:, :margin] = edge
        ref[:, ref.shape[1] - margin :] = edge
        ref[:, margin : ref.shape[1] - margin] = value
    else:
        ref[...] = value


def drift(x, embed, w_in, w_mid, w_out, first_row, total_rows, same):
    steps_dev, rows_in, columns, channels = x.shape
    hidden = w_in.shape[1]
    margin = 1 if same else 0
    rows_1 = rows_in - 2
    rows_2 = rows_1 + 2 * margin - 2
    rows_3 = rows_2 + 2 * margin - 2
    w1, w2, w3 = w_in.T, w_mid.T, w_out.T
    flops = 2 * steps_dev * columns * 9 * hidden * (channels * rows_1 + hidden * rows_2 + channels * rows_3)
    vmem = pl.BlockSpec(memory_space=pltpu.VMEM)
    out = pl.pallas_call(
        lambda *refs: drift_kernel(total_rows, same, *refs),
        out_shape=jax.ShapeDtypeStruct((steps_dev, rows_3, columns, channels), jnp.float32),
        in_specs=[pl.BlockSpec(memory_space=pltpu.SMEM)] + [vmem] * 5,
        out_specs=vmem,
        scratch_shapes=[
            pltpu.VMEM((steps_dev, rows_1 + 2 * margin, columns, hidden), jnp.bfloat16),
            pltpu.VMEM((steps_dev, rows_2 + 2 * margin, columns, hidden), jnp.bfloat16),
        ],
        compiler_params=pltpu.CompilerParams(vmem_limit_bytes=48 * 1024 * 1024),
        cost_estimate=pl.CostEstimate(
            flops=flops,
            transcendentals=steps_dev * columns * hidden * (rows_1 + rows_2),
            bytes_accessed=2 * (w1.size + w2.size + w3.size) + 2 * x.size + 4 * steps_dev * rows_3 * columns * channels,
        ),
    )(jnp.reshape(first_row, (1,)).astype(jnp.int32), x, embed, w1, w2, w3)
    return out.reshape(steps_dev, rows_3, columns * channels)


def shifted(array, by):
    devices = lax.axis_size(TIME_AXES)
    pairs = [(i, i + by) for i in range(devices - by)]
    return lax.ppermute(array, TIME_AXES, pairs)


def scan_earlier(total, carried):
    devices = lax.axis_size(TIME_AXES)
    radix = min(devices, 8)
    earlier = None
    window = total
    moved = None
    stride = 1
    while stride < devices:
        got_all = []
        for k in range(1, radix):
            by = k * stride
            if by >= devices:
                break
            if by == 1 and carried is not None:
                both = shifted(jnp.stack([window, carried]), 1)
                got, moved = both[0], both[1]
            else:
                got = shifted(window, by)
            got_all.append(got)
        gathered = got_all[0]
        for got in got_all[1:]:
            gathered = gathered + got
        earlier = gathered if earlier is None else earlier + gathered
        stride *= radix
        if stride < devices:
            window = window + gathered
    return earlier, moved


def shards(start_state, guess, w_in, w_mid, w_out, time_embed, levels, plan, offset):
    steps_dev = guess.shape[0]
    devices = lax.axis_size(TIME_AXES)
    time_index = lax.axis_index(TIME_AXES)
    first_step = time_index * steps_dev
    window_ids = lax.dynamic_slice_in_dim(plan, offset[0] + first_step, steps_dev + 1)
    after_id = lax.dynamic_slice_in_dim(
        plan, jnp.minimum(offset[0] + first_step + steps_dev + 1, plan.shape[0] - 1), 1
    )
    all_ids = jnp.concatenate([window_ids, after_id])
    one_hot = all_ids[:, None] == jnp.arange(levels.shape[0], dtype=jnp.int32)[None, :]
    noise = jnp.dot(one_hot.astype(jnp.float32), levels, precision=lax.Precision.HIGHEST)
    step_size = noise[1 : steps_dev + 1] - noise[:steps_dev]
    next_step = jnp.where(time_index < devices - 1, noise[steps_dev + 1] - noise[steps_dev], 0.0)
    embed = jnp.dot(
        one_hot[:steps_dev].astype(jnp.bfloat16), time_embed, preferred_element_type=jnp.float32
    )
    factor = jnp.where(first_step + jnp.arange(steps_dev, dtype=jnp.int32) == 0, 1.0, 1.5).astype(
        jnp.float32
    )
    channels = w_out.shape[1]
    tile_rows = guess.shape[1]
    columns = guess.shape[2] // channels
    chan = lax.axis_index("chan")
    total_rows = tile_rows * lax.axis_size("chan")
    whole_tile = lax.axis_size("chan") == 2

    def tiles(block, rows):
        return block.reshape(steps_dev, rows, columns, channels)

    def sweep_step(drift_now, carry_last):
        earlier_local = jnp.concatenate([jnp.zeros_like(drift_now[:1]), drift_now[:-1]], axis=0)
        increment = step_size[:, None, None] * (factor[:, None, None] * drift_now - 0.5 * earlier_local)
        running = jnp.cumsum(increment, axis=0)
        handed_on = running[-1] - 0.5 * next_step * drift_now[-1]
        earlier_sum, previous = scan_earlier(handed_on, drift_now[-1] if carry_last else None)
        return increment, running, earlier_sum, previous

    def before_of(start, increment, running, earlier_sum, previous):
        states_before = (start + earlier_sum)[None] + running - increment
        return states_before.at[0].add(0.5 * step_size[0] * previous)

    if whole_tile:
        own = jnp.concatenate([start_state[None], guess.astype(jnp.float32)], axis=0)
        other = lax.ppermute(own, "chan", [(0, 1), (1, 0)])
        full = jnp.where(chan == 0, jnp.concatenate([own, other], axis=1), jnp.concatenate([other, own], axis=1))
        start_full = full[0]
        layer_full = full[1:].astype(jnp.bfloat16)
        for sweep in range(ITERS - 1):
            x = jnp.pad(tiles(layer_full, total_rows), ((0, 0), (1, 1), (0, 0), (0, 0)))
            drift_now = drift(x, embed, w_in, w_mid, w_out, jnp.int32(0), total_rows, True)
            parts = sweep_step(drift_now, True)
            layer_full = before_of(start_full, *parts).astype(jnp.bfloat16)
        padded = jnp.pad(layer_full, ((0, 0), (3, 3), (0, 0)))
        rimmed = lax.dynamic_slice_in_dim(padded, chan * tile_rows, tile_rows + 6, axis=1)
    else:
        layer_in = guess
        for sweep in range(ITERS - 1):
            rimmed = padded_2(layer_in, (("chan", 1),), 3)
            drift_now = drift(tiles(rimmed, tile_rows + 6), embed, w_in, w_mid, w_out, chan * tile_rows - 2, total_rows, False)
            parts = sweep_step(drift_now, True)
            layer_in = before_of(start_state, *parts).astype(jnp.bfloat16)
        rimmed = padded_2(layer_in, (("chan", 1),), 3)
    drift_now = drift(tiles(rimmed, tile_rows + 6), embed, w_in, w_mid, w_out, chan * tile_rows - 2, total_rows, False)
    increment, running, earlier_sum, _ = sweep_step(drift_now, False)
    return (start_state + earlier_sum)[None] + running


def solution(mesh):
    return jax.shard_map(
        shards,
        mesh=mesh,
        in_specs=(
            P(("parts", "chan"), None),
            P(("parts", "tm", "sub"), "chan", None),
            P(),
            P(),
            P(),
            P(),
            P(),
            P("parts"),
            P("parts"),
        ),
        out_specs=P(("parts", "tm", "sub"), "chan", None),
        check_vma=False,
    )
```

```python
import jax
import jax.numpy as jnp
from jax import lax
from jax.experimental import pallas as pl
from jax.experimental.pallas import tpu as pltpu
from jax.sharding import PartitionSpec as P

ITERS = 2
TIME_AXES = ("tm", "sub")


def padded_2(block, sides, width):
    for axis, dim in sides:
        count = lax.axis_size(axis)
        forward = [(i, i + 1) for i in range(count - 1)]
        backward = [(target, source) for source, target in forward]
        low = lax.ppermute(
            lax.slice_in_dim(block, block.shape[dim] - width, None, axis=dim), axis, forward
        )
        high = lax.ppermute(lax.slice_in_dim(block, 0, width, axis=dim), axis, backward)
        block = jnp.concatenate([low, block, high], axis=dim)
    return block


def conv3x3(src_ref, w_ref, rows_out):
    steps, _, columns, channels_in = src_ref.shape
    channels_out = w_ref.shape[0]
    size = steps * rows_out * columns
    taps = []
    for col_off in range(3):
        acc = None
        for row_off in range(3):
            patch = src_ref[:, row_off : row_off + rows_out].reshape(size, channels_in)
            tap = row_off * 3 + col_off
            weight = w_ref[:, tap * channels_in : (tap + 1) * channels_in]
            part = lax.dot_general(
                patch, weight, (((1,), (1,)), ((), ())), preferred_element_type=jnp.float32
            )
            acc = part if acc is None else acc + part
        taps.append(acc)
    column = lax.broadcasted_iota(jnp.int32, (steps * rows_out, columns, channels_out), 1)
    column = column.reshape(size, channels_out)
    left = jnp.where(column == 0, 0.0, pltpu.roll(taps[0], 1, 0))
    right = jnp.where(column == columns - 1, 0.0, pltpu.roll(taps[2], size - 1, 0))
    return (left + taps[1] + right).reshape(steps, rows_out, columns, channels_out)


def silu(v):
    return v / (1.0 + jnp.exp(-v))


def row_valid(shape, first_row, total_rows):
    rows = first_row + lax.broadcasted_iota(jnp.int32, shape, 1)
    return (rows >= 0) & (rows < total_rows)


def drift_kernel(total_rows, same, first_ref, x_ref, emb_ref, w1_ref, w2_ref, w3_ref, out_ref, h1_ref, h2_ref):
    first_row = first_ref[0]
    margin = 1 if same else 0
    rows_1 = h1_ref.shape[1] - 2 * margin
    rows_2 = h2_ref.shape[1] - 2 * margin
    act = conv3x3(x_ref, w1_ref, rows_1) + emb_ref[...][:, None, None, :]
    act = jnp.where(row_valid(act.shape, first_row, total_rows), silu(act), 0.0)
    store_hidden(h1_ref, act.astype(jnp.bfloat16), margin)
    act = conv3x3(h1_ref, w2_ref, rows_2)
    act = jnp.where(row_valid(act.shape, first_row + 1 - margin, total_rows), silu(act), 0.0)
    store_hidden(h2_ref, act.astype(jnp.bfloat16), margin)
    out_ref[...] = conv3x3(h2_ref, w3_ref, out_ref.shape[1])


def store_hidden(ref, value, margin):
    if margin:
        edge = jnp.zeros((ref.shape[0], margin) + ref.shape[2:], ref.dtype)
        ref[:, :margin] = edge
        ref[:, ref.shape[1] - margin :] = edge
        ref[:, margin : ref.shape[1] - margin] = value
    else:
        ref[...] = value


def drift(x, embed, w_in, w_mid, w_out, first_row, total_rows, same):
    steps_dev, rows_in, columns, channels = x.shape
    hidden = w_in.shape[1]
    margin = 1 if same else 0
    rows_1 = rows_in - 2
    rows_2 = rows_1 + 2 * margin - 2
    rows_3 = rows_2 + 2 * margin - 2
    w1, w2, w3 = w_in.T, w_mid.T, w_out.T
    flops = 2 * steps_dev * columns * 9 * hidden * (channels * rows_1 + hidden * rows_2 + channels * rows_3)
    vmem = pl.BlockSpec(memory_space=pltpu.VMEM)
    out = pl.pallas_call(
        lambda *refs: drift_kernel(total_rows, same, *refs),
        out_shape=jax.ShapeDtypeStruct((steps_dev, rows_3, columns, channels), jnp.float32),
        in_specs=[pl.BlockSpec(memory_space=pltpu.SMEM)] + [vmem] * 5,
        out_specs=vmem,
        scratch_shapes=[
            pltpu.VMEM((steps_dev, rows_1 + 2 * margin, columns, hidden), jnp.bfloat16),
            pltpu.VMEM((steps_dev, rows_2 + 2 * margin, columns, hidden), jnp.bfloat16),
        ],
        compiler_params=pltpu.CompilerParams(vmem_limit_bytes=48 * 1024 * 1024),
        cost_estimate=pl.CostEstimate(
            flops=flops,
            transcendentals=steps_dev * columns * hidden * (rows_1 + rows_2),
            bytes_accessed=2 * (w1.size + w2.size + w3.size) + 2 * x.size + 4 * steps_dev * rows_3 * columns * channels,
        ),
    )(jnp.reshape(first_row, (1,)).astype(jnp.int32), x, embed, w1, w2, w3)
    return out


def shifted(array, by):
    devices = lax.axis_size(TIME_AXES)
    pairs = [(i, i + by) for i in range(devices - by)]
    return lax.ppermute(array, TIME_AXES, pairs)


def scan_earlier(total, carried):
    devices = lax.axis_size(TIME_AXES)
    radix = min(devices, 8)
    earlier = None
    window = total
    moved = None
    stride = 1
    while stride < devices:
        got_all = []
        for k in range(1, radix):
            by = k * stride
            if by >= devices:
                break
            if by == 1 and carried is not None:
                both = shifted(jnp.stack([window, carried]), 1)
                got, moved = both[0], both[1]
            else:
                got = shifted(window, by)
            got_all.append(got)
        gathered = got_all[0]
        for got in got_all[1:]:
            gathered = gathered + got
        earlier = gathered if earlier is None else earlier + gathered
        stride *= radix
        if stride < devices:
            window = window + gathered
    return earlier, moved


def shards(start_state, guess, w_in, w_mid, w_out, time_embed, levels, plan, offset):
    steps_dev = guess.shape[0]
    devices = lax.axis_size(TIME_AXES)
    time_index = lax.axis_index(TIME_AXES)
    first_step = time_index * steps_dev
    window_ids = lax.dynamic_slice_in_dim(plan, offset[0] + first_step, steps_dev + 1)
    after_id = lax.dynamic_slice_in_dim(
        plan, jnp.minimum(offset[0] + first_step + steps_dev + 1, plan.shape[0] - 1), 1
    )
    all_ids = jnp.concatenate([window_ids, after_id])
    one_hot = all_ids[:, None] == jnp.arange(levels.shape[0], dtype=jnp.int32)[None, :]
    noise = jnp.dot(one_hot.astype(jnp.float32), levels, precision=lax.Precision.HIGHEST)
    step_size = noise[1 : steps_dev + 1] - noise[:steps_dev]
    next_step = jnp.where(time_index < devices - 1, noise[steps_dev + 1] - noise[steps_dev], 0.0)
    embed = jnp.dot(
        one_hot[:steps_dev].astype(jnp.bfloat16), time_embed, preferred_element_type=jnp.float32
    )
    factor = jnp.where(first_step + jnp.arange(steps_dev, dtype=jnp.int32) == 0, 1.0, 1.5).astype(
        jnp.float32
    )
    channels = w_out.shape[1]
    tile_rows = guess.shape[1]
    columns = guess.shape[2] // channels
    chan = lax.axis_index("chan")
    total_rows = tile_rows * lax.axis_size("chan")
    whole_tile = lax.axis_size("chan") == 2

    start4 = start_state.reshape(tile_rows, columns, channels)
    guess4 = guess.reshape(steps_dev, tile_rows, columns, channels)
    per_step = lambda v: v[:, None, None, None]

    def sweep_step(drift_now, carry_last):
        earlier_local = jnp.concatenate([jnp.zeros_like(drift_now[:1]), drift_now[:-1]], axis=0)
        increment = per_step(step_size) * (per_step(factor) * drift_now - 0.5 * earlier_local)
        running = jnp.cumsum(increment, axis=0)
        handed_on = running[-1] - 0.5 * next_step * drift_now[-1]
        earlier_sum, previous = scan_earlier(handed_on, drift_now[-1] if carry_last else None)
        return increment, running, earlier_sum, previous

    def before_of(start, increment, running, earlier_sum, previous):
        states_before = (start + earlier_sum)[None] + running - increment
        return states_before.at[0].add(0.5 * step_size[0] * previous)

    if whole_tile:
        own = jnp.concatenate([start4[None], guess4.astype(jnp.float32)], axis=0)
        other = lax.ppermute(own, "chan", [(0, 1), (1, 0)])
        full = jnp.where(chan == 0, jnp.concatenate([own, other], axis=1), jnp.concatenate([other, own], axis=1))
        start_full = full[0]
        layer_full = full[1:].astype(jnp.bfloat16)
        for sweep in range(ITERS - 1):
            x = jnp.pad(layer_full, ((0, 0), (1, 1), (0, 0), (0, 0)))
            drift_now = drift(x, embed, w_in, w_mid, w_out, jnp.int32(0), total_rows, True)
            parts = sweep_step(drift_now, True)
            layer_full = before_of(start_full, *parts).astype(jnp.bfloat16)
        padded = jnp.pad(layer_full, ((0, 0), (3, 3), (0, 0), (0, 0)))
        rimmed = lax.dynamic_slice_in_dim(padded, chan * tile_rows, tile_rows + 6, axis=1)
    else:
        layer_in = guess4
        for sweep in range(ITERS - 1):
            rimmed = padded_2(layer_in, (("chan", 1),), 3)
            drift_now = drift(rimmed, embed, w_in, w_mid, w_out, chan * tile_rows - 2, total_rows, False)
            parts = sweep_step(drift_now, True)
            layer_in = before_of(start4, *parts).astype(jnp.bfloat16)
        rimmed = padded_2(layer_in, (("chan", 1),), 3)
    drift_now = drift(rimmed, embed, w_in, w_mid, w_out, chan * tile_rows - 2, total_rows, False)
    increment, running, earlier_sum, _ = sweep_step(drift_now, False)
    states_after = (start4 + earlier_sum)[None] + running
    return states_after.reshape(guess.shape)


def solution(mesh):
    return jax.shard_map(
        shards,
        mesh=mesh,
        in_specs=(
            P(("parts", "chan"), None),
            P(("parts", "tm", "sub"), "chan", None),
            P(),
            P(),
            P(),
            P(),
            P(),
            P("parts"),
            P("parts"),
        ),
        out_specs=P(("parts", "tm", "sub"), "chan", None),
        check_vma=False,
    )
```

```python
import jax
import jax.numpy as jnp
from jax import lax
from jax.experimental import pallas as pl
from jax.experimental.pallas import tpu as pltpu
from jax.sharding import PartitionSpec as P

ITERS = 2
TIME_AXES = ("tm", "sub")


def padded_2(block, sides, width):
    for axis, dim in sides:
        count = lax.axis_size(axis)
        forward = [(i, i + 1) for i in range(count - 1)]
        backward = [(target, source) for source, target in forward]
        low = lax.ppermute(
            lax.slice_in_dim(block, block.shape[dim] - width, None, axis=dim), axis, forward
        )
        high = lax.ppermute(lax.slice_in_dim(block, 0, width, axis=dim), axis, backward)
        block = jnp.concatenate([low, block, high], axis=dim)
    return block


def conv3x3(src_ref, w_ref, rows_out):
    steps, _, columns, channels_in = src_ref.shape
    channels_out = w_ref.shape[0]
    size = steps * rows_out * columns
    taps = []
    for col_off in range(3):
        acc = None
        for row_off in range(3):
            patch = src_ref[:, row_off : row_off + rows_out].reshape(size, channels_in)
            tap = row_off * 3 + col_off
            weight = w_ref[:, tap * channels_in : (tap + 1) * channels_in]
            part = lax.dot_general(
                patch, weight, (((1,), (1,)), ((), ())), preferred_element_type=jnp.float32
            )
            acc = part if acc is None else acc + part
        taps.append(acc)
    column = lax.broadcasted_iota(jnp.int32, (steps * rows_out, columns, channels_out), 1)
    column = column.reshape(size, channels_out)
    left = jnp.where(column == 0, 0.0, pltpu.roll(taps[0], 1, 0))
    right = jnp.where(column == columns - 1, 0.0, pltpu.roll(taps[2], size - 1, 0))
    return (left + taps[1] + right).reshape(steps, rows_out, columns, channels_out)


def silu(v):
    return v / (1.0 + jnp.exp(-v))


def row_valid(shape, first_row, total_rows):
    rows = first_row + lax.broadcasted_iota(jnp.int32, shape, 1)
    return (rows >= 0) & (rows < total_rows)


def drift_kernel(total_rows, same, first_ref, x_ref, emb_ref, w1_ref, w2_ref, w3_ref, out_ref, h1_ref, h2_ref):
    first_row = first_ref[0]
    margin = 1 if same else 0
    rows_1 = h1_ref.shape[1] - 2 * margin
    rows_2 = h2_ref.shape[1] - 2 * margin
    act = conv3x3(x_ref, w1_ref, rows_1) + emb_ref[...][:, None, None, :]
    act = jnp.where(row_valid(act.shape, first_row, total_rows), silu(act), 0.0)
    store_hidden(h1_ref, act.astype(jnp.bfloat16), margin)
    act = conv3x3(h1_ref, w2_ref, rows_2)
    act = jnp.where(row_valid(act.shape, first_row + 1 - margin, total_rows), silu(act), 0.0)
    store_hidden(h2_ref, act.astype(jnp.bfloat16), margin)
    out_ref[...] = conv3x3(h2_ref, w3_ref, out_ref.shape[1])


def store_hidden(ref, value, margin):
    if margin:
        edge = jnp.zeros((ref.shape[0], margin) + ref.shape[2:], ref.dtype)
        ref[:, :margin] = edge
        ref[:, ref.shape[1] - margin :] = edge
        ref[:, margin : ref.shape[1] - margin] = value
    else:
        ref[...] = value


def drift(x, embed, w_in, w_mid, w_out, first_row, total_rows, same):
    steps_dev, rows_in, columns, channels = x.shape
    hidden = w_in.shape[1]
    margin = 1 if same else 0
    rows_1 = rows_in - 2
    rows_2 = rows_1 + 2 * margin - 2
    rows_3 = rows_2 + 2 * margin - 2
    w1, w2, w3 = w_in.T, w_mid.T, w_out.T
    flops = 2 * steps_dev * columns * 9 * hidden * (channels * rows_1 + hidden * rows_2 + channels * rows_3)
    vmem = pl.BlockSpec(memory_space=pltpu.VMEM)
    out = pl.pallas_call(
        lambda *refs: drift_kernel(total_rows, same, *refs),
        out_shape=jax.ShapeDtypeStruct((steps_dev, rows_3, columns, channels), jnp.float32),
        in_specs=[pl.BlockSpec(memory_space=pltpu.SMEM)] + [vmem] * 5,
        out_specs=vmem,
        scratch_shapes=[
            pltpu.VMEM((steps_dev, rows_1 + 2 * margin, columns, hidden), jnp.bfloat16),
            pltpu.VMEM((steps_dev, rows_2 + 2 * margin, columns, hidden), jnp.bfloat16),
        ],
        compiler_params=pltpu.CompilerParams(vmem_limit_bytes=48 * 1024 * 1024),
        cost_estimate=pl.CostEstimate(
            flops=flops,
            transcendentals=steps_dev * columns * hidden * (rows_1 + rows_2),
            bytes_accessed=2 * (w1.size + w2.size + w3.size) + 2 * x.size + 4 * steps_dev * rows_3 * columns * channels,
        ),
    )(jnp.reshape(first_row, (1,)).astype(jnp.int32), x, embed, w1, w2, w3)
    return lax.optimization_barrier(out.reshape(steps_dev, rows_3, columns * channels))


def shifted(array, by):
    devices = lax.axis_size(TIME_AXES)
    pairs = [(i, i + by) for i in range(devices - by)]
    return lax.ppermute(array, TIME_AXES, pairs)


def scan_earlier(total, carried):
    devices = lax.axis_size(TIME_AXES)
    radix = min(devices, 8)
    earlier = None
    window = total
    moved = None
    stride = 1
    while stride < devices:
        got_all = []
        for k in range(1, radix):
            by = k * stride
            if by >= devices:
                break
            if by == 1 and carried is not None:
                both = shifted(jnp.stack([window, carried]), 1)
                got, moved = both[0], both[1]
            else:
                got = shifted(window, by)
            got_all.append(got)
        gathered = got_all[0]
        for got in got_all[1:]:
            gathered = gathered + got
        earlier = gathered if earlier is None else earlier + gathered
        stride *= radix
        if stride < devices:
            window = window + gathered
    return earlier, moved


def shards(start_state, guess, w_in, w_mid, w_out, time_embed, levels, plan, offset):
    steps_dev = guess.shape[0]
    devices = lax.axis_size(TIME_AXES)
    time_index = lax.axis_index(TIME_AXES)
    first_step = time_index * steps_dev
    positions = offset[0] + first_step + jnp.arange(steps_dev + 2, dtype=jnp.int32)
    picked = positions[:, None] == jnp.arange(plan.shape[0], dtype=jnp.int32)[None, :]
    all_ids = jnp.sum(jnp.where(picked, plan[None, :], 0), axis=1)
    one_hot = all_ids[:, None] == jnp.arange(levels.shape[0], dtype=jnp.int32)[None, :]
    noise = jnp.dot(one_hot.astype(jnp.float32), levels, precision=lax.Precision.HIGHEST)
    step_size = noise[1 : steps_dev + 1] - noise[:steps_dev]
    next_step = jnp.where(time_index < devices - 1, noise[steps_dev + 1] - noise[steps_dev], 0.0)
    embed = jnp.dot(
        one_hot[:steps_dev].astype(jnp.bfloat16), time_embed, preferred_element_type=jnp.float32
    )
    factor = jnp.where(first_step + jnp.arange(steps_dev, dtype=jnp.int32) == 0, 1.0, 1.5).astype(
        jnp.float32
    )
    channels = w_out.shape[1]
    tile_rows = guess.shape[1]
    columns = guess.shape[2] // channels
    chan = lax.axis_index("chan")
    total_rows = tile_rows * lax.axis_size("chan")
    whole_tile = lax.axis_size("chan") == 2

    def tiles(block, rows):
        return block.reshape(steps_dev, rows, columns, channels)

    def sweep_step(drift_now, carry_last):
        earlier_local = jnp.concatenate([jnp.zeros_like(drift_now[:1]), drift_now[:-1]], axis=0)
        increment = step_size[:, None, None] * (factor[:, None, None] * drift_now - 0.5 * earlier_local)
        running = jnp.cumsum(increment, axis=0)
        handed_on = running[-1] - 0.5 * next_step * drift_now[-1]
        earlier_sum, previous = scan_earlier(handed_on, drift_now[-1] if carry_last else None)
        return increment, running, earlier_sum, previous

    def before_of(start, increment, running, earlier_sum, previous):
        states_before = (start + earlier_sum)[None] + running - increment
        return states_before.at[0].add(0.5 * step_size[0] * previous)

    if whole_tile:
        own = jnp.concatenate([start_state[None], guess.astype(jnp.float32)], axis=0)
        other = lax.ppermute(own, "chan", [(0, 1), (1, 0)])
        full = jnp.where(chan == 0, jnp.concatenate([own, other], axis=1), jnp.concatenate([other, own], axis=1))
        start_full = full[0]
        layer_full = full[1:].astype(jnp.bfloat16)
        for sweep in range(ITERS - 1):
            x = jnp.pad(tiles(layer_full, total_rows), ((0, 0), (1, 1), (0, 0), (0, 0)))
            drift_now = drift(x, embed, w_in, w_mid, w_out, jnp.int32(0), total_rows, True)
            parts = sweep_step(drift_now, True)
            layer_full = before_of(start_full, *parts).astype(jnp.bfloat16)
        padded = jnp.pad(layer_full, ((0, 0), (3, 3), (0, 0)))
        rimmed = lax.dynamic_slice_in_dim(padded, chan * tile_rows, tile_rows + 6, axis=1)
    else:
        layer_in = guess
        for sweep in range(ITERS - 1):
            rimmed = padded_2(layer_in, (("chan", 1),), 3)
            drift_now = drift(tiles(rimmed, tile_rows + 6), embed, w_in, w_mid, w_out, chan * tile_rows - 2, total_rows, False)
            parts = sweep_step(drift_now, True)
            layer_in = before_of(start_state, *parts).astype(jnp.bfloat16)
        rimmed = padded_2(layer_in, (("chan", 1),), 3)
    drift_now = drift(tiles(rimmed, tile_rows + 6), embed, w_in, w_mid, w_out, chan * tile_rows - 2, total_rows, False)
    increment, running, earlier_sum, _ = sweep_step(drift_now, False)
    return (start_state + earlier_sum)[None] + running


def solution(mesh):
    return jax.shard_map(
        shards,
        mesh=mesh,
        in_specs=(
            P(("parts", "chan"), None),
            P(("parts", "tm", "sub"), "chan", None),
            P(),
            P(),
            P(),
            P(),
            P(),
            P("parts"),
            P("parts"),
        ),
        out_specs=P(("parts", "tm", "sub"), "chan", None),
        check_vma=False,
    )
```

```python
import jax
import jax.numpy as jnp
from jax import lax
from jax.experimental import pallas as pl
from jax.experimental.pallas import tpu as pltpu
from jax.sharding import PartitionSpec as P

ITERS = 2
TIME_AXES = ("tm", "sub")


def padded_2(block, sides, width):
    for axis, dim in sides:
        count = lax.axis_size(axis)
        forward = [(i, i + 1) for i in range(count - 1)]
        backward = [(target, source) for source, target in forward]
        low = lax.ppermute(
            lax.slice_in_dim(block, block.shape[dim] - width, None, axis=dim), axis, forward
        )
        high = lax.ppermute(lax.slice_in_dim(block, 0, width, axis=dim), axis, backward)
        block = jnp.concatenate([low, block, high], axis=dim)
    return block


def conv3x3(src_ref, w_ref, rows_out):
    steps, _, columns, channels_in = src_ref.shape
    channels_out = w_ref.shape[0]
    size = steps * rows_out * columns
    taps = []
    for col_off in range(3):
        acc = None
        for row_off in range(3):
            patch = src_ref[:, row_off : row_off + rows_out].reshape(size, channels_in)
            tap = row_off * 3 + col_off
            weight = w_ref[:, tap * channels_in : (tap + 1) * channels_in]
            part = lax.dot_general(
                patch, weight, (((1,), (1,)), ((), ())), preferred_element_type=jnp.float32
            )
            acc = part if acc is None else acc + part
        taps.append(acc)
    column = lax.broadcasted_iota(jnp.int32, (steps * rows_out, columns, channels_out), 1)
    column = column.reshape(size, channels_out)
    left = jnp.where(column == 0, 0.0, pltpu.roll(taps[0], 1, 0))
    right = jnp.where(column == columns - 1, 0.0, pltpu.roll(taps[2], size - 1, 0))
    return (left + taps[1] + right).reshape(steps, rows_out, columns, channels_out)


def silu(v):
    return v / (1.0 + jnp.exp(-v))


def row_valid(shape, first_row, total_rows):
    rows = first_row + lax.broadcasted_iota(jnp.int32, shape, 1)
    return (rows >= 0) & (rows < total_rows)


def drift_kernel(total_rows, same, first_ref, x_ref, emb_ref, w1_ref, w2_ref, w3_ref, out_ref, h1_ref, h2_ref):
    first_row = first_ref[0]
    margin = 1 if same else 0
    rows_1 = h1_ref.shape[1] - 2 * margin
    rows_2 = h2_ref.shape[1] - 2 * margin
    act = conv3x3(x_ref, w1_ref, rows_1) + emb_ref[...][:, None, None, :]
    act = jnp.where(row_valid(act.shape, first_row, total_rows), silu(act), 0.0)
    store_hidden(h1_ref, act.astype(jnp.bfloat16), margin)
    act = conv3x3(h1_ref, w2_ref, rows_2)
    act = jnp.where(row_valid(act.shape, first_row + 1 - margin, total_rows), silu(act), 0.0)
    store_hidden(h2_ref, act.astype(jnp.bfloat16), margin)
    out_ref[...] = conv3x3(h2_ref, w3_ref, out_ref.shape[1])


def store_hidden(ref, value, margin):
    if margin:
        edge = jnp.zeros((ref.shape[0], margin) + ref.shape[2:], ref.dtype)
        ref[:, :margin] = edge
        ref[:, ref.shape[1] - margin :] = edge
        ref[:, margin : ref.shape[1] - margin] = value
    else:
        ref[...] = value


def drift(x, embed, w_in, w_mid, w_out, first_row, total_rows, same):
    steps_dev, rows_in, columns, channels = x.shape
    hidden = w_in.shape[1]
    margin = 1 if same else 0
    rows_1 = rows_in - 2
    rows_2 = rows_1 + 2 * margin - 2
    rows_3 = rows_2 + 2 * margin - 2
    w1, w2, w3 = w_in.T, w_mid.T, w_out.T
    flops = 2 * steps_dev * columns * 9 * hidden * (channels * rows_1 + hidden * rows_2 + channels * rows_3)
    vmem = pl.BlockSpec(memory_space=pltpu.VMEM)
    out = pl.pallas_call(
        lambda *refs: drift_kernel(total_rows, same, *refs),
        out_shape=jax.ShapeDtypeStruct((steps_dev, rows_3, columns, channels), jnp.float32),
        in_specs=[pl.BlockSpec(memory_space=pltpu.SMEM)] + [vmem] * 5,
        out_specs=vmem,
        scratch_shapes=[
            pltpu.VMEM((steps_dev, rows_1 + 2 * margin, columns, hidden), jnp.bfloat16),
            pltpu.VMEM((steps_dev, rows_2 + 2 * margin, columns, hidden), jnp.bfloat16),
        ],
        compiler_params=pltpu.CompilerParams(vmem_limit_bytes=48 * 1024 * 1024),
        cost_estimate=pl.CostEstimate(
            flops=flops,
            transcendentals=steps_dev * columns * hidden * (rows_1 + rows_2),
            bytes_accessed=2 * (w1.size + w2.size + w3.size) + 2 * x.size + 4 * steps_dev * rows_3 * columns * channels,
        ),
    )(jnp.reshape(first_row, (1,)).astype(jnp.int32), x, embed, w1, w2, w3)
    return lax.optimization_barrier(out.reshape(steps_dev, rows_3, columns * channels))


def shifted(array, by):
    devices = lax.axis_size(TIME_AXES)
    pairs = [(i, i + by) for i in range(devices - by)]
    return lax.ppermute(array, TIME_AXES, pairs)


def scan_earlier(total, carried):
    devices = lax.axis_size(TIME_AXES)
    radix = min(devices, 8)
    earlier = None
    window = total
    moved = None
    stride = 1
    while stride < devices:
        got_all = []
        for k in range(1, radix):
            by = k * stride
            if by >= devices:
                break
            if by == 1 and carried is not None:
                both = shifted(jnp.stack([window, carried]), 1)
                got, moved = both[0], both[1]
            else:
                got = shifted(window, by)
            got_all.append(got)
        gathered = got_all[0]
        for got in got_all[1:]:
            gathered = gathered + got
        earlier = gathered if earlier is None else earlier + gathered
        stride *= radix
        if stride < devices:
            window = window + gathered
    return earlier, moved


def shards(start_state, guess, w_in, w_mid, w_out, time_embed, levels, plan, offset):
    steps_dev = guess.shape[0]
    devices = lax.axis_size(TIME_AXES)
    time_index = lax.axis_index(TIME_AXES)
    first_step = time_index * steps_dev
    positions = offset[0] + first_step + jnp.arange(steps_dev + 2, dtype=jnp.int32)
    picked = positions[:, None] == jnp.arange(plan.shape[0], dtype=jnp.int32)[None, :]
    all_ids = jnp.sum(jnp.where(picked, plan[None, :], 0), axis=1)
    one_hot = all_ids[:, None] == jnp.arange(levels.shape[0], dtype=jnp.int32)[None, :]
    noise = jnp.dot(one_hot.astype(jnp.float32), levels, precision=lax.Precision.HIGHEST)
    step_size = noise[1 : steps_dev + 1] - noise[:steps_dev]
    next_step = jnp.where(time_index < devices - 1, noise[steps_dev + 1] - noise[steps_dev], 0.0)
    embed = jnp.dot(
        one_hot[:steps_dev].astype(jnp.bfloat16), time_embed, preferred_element_type=jnp.float32
    )
    factor = jnp.where(first_step + jnp.arange(steps_dev, dtype=jnp.int32) == 0, 1.0, 1.5).astype(
        jnp.float32
    )
    channels = w_out.shape[1]
    tile_rows = guess.shape[1]
    columns = guess.shape[2] // channels
    chan = lax.axis_index("chan")
    total_rows = tile_rows * lax.axis_size("chan")
    whole_tile = lax.axis_size("chan") == 2

    def tiles(block, rows):
        return block.reshape(steps_dev, rows, columns, channels)

    step_after = jnp.concatenate([step_size[1:], next_step[None]])
    weight_on = step_size * factor - 0.5 * step_after

    def sweep_step(drift_now, carry_last):
        handed_on = jnp.sum(weight_on[:, None, None] * drift_now, axis=0)
        earlier_sum, previous = scan_earlier(handed_on, drift_now[-1] if carry_last else None)
        return drift_now, earlier_sum, previous

    def increments(drift_now):
        return [
            step_size[n] * (factor[n] * drift_now[n] - (0.5 * drift_now[n - 1] if n else 0.0))
            for n in range(steps_dev)
        ]

    def before_of(start, drift_now, earlier_sum, previous):
        level = start + earlier_sum
        states = [level + 0.5 * step_size[0] * previous]
        for inc in increments(drift_now)[:-1]:
            level = level + inc
            states.append(level)
        return jnp.stack(states)

    if whole_tile:
        swap = [(0, 1), (1, 0)]
        other_start = lax.ppermute(start_state, "chan", swap)
        other_guess = lax.ppermute(guess, "chan", swap)
        in_order = lambda mine, theirs, axis: jnp.where(
            chan == 0, jnp.concatenate([mine, theirs], axis=axis), jnp.concatenate([theirs, mine], axis=axis)
        )
        start_full = in_order(start_state, other_start, 0)
        layer_full = in_order(guess, other_guess, 1)
        for sweep in range(ITERS - 1):
            x = jnp.pad(tiles(layer_full, total_rows), ((0, 0), (1, 1), (0, 0), (0, 0)))
            drift_now = drift(x, embed, w_in, w_mid, w_out, jnp.int32(0), total_rows, True)
            parts = sweep_step(drift_now, True)
            layer_full = before_of(start_full, *parts).astype(jnp.bfloat16)
        padded = jnp.pad(layer_full, ((0, 0), (3, 3), (0, 0)))
        rimmed = lax.dynamic_slice_in_dim(padded, chan * tile_rows, tile_rows + 6, axis=1)
    else:
        layer_in = guess
        for sweep in range(ITERS - 1):
            rimmed = padded_2(layer_in, (("chan", 1),), 3)
            drift_now = drift(tiles(rimmed, tile_rows + 6), embed, w_in, w_mid, w_out, chan * tile_rows - 2, total_rows, False)
            parts = sweep_step(drift_now, True)
            layer_in = before_of(start_state, *parts).astype(jnp.bfloat16)
        rimmed = padded_2(layer_in, (("chan", 1),), 3)
    drift_now = drift(tiles(rimmed, tile_rows + 6), embed, w_in, w_mid, w_out, chan * tile_rows - 2, total_rows, False)
    _, earlier_sum, _ = sweep_step(drift_now, False)
    running = jnp.cumsum(jnp.stack(increments(drift_now)), axis=0)
    return (start_state + earlier_sum)[None] + running


def solution(mesh):
    return jax.shard_map(
        shards,
        mesh=mesh,
        in_specs=(
            P(("parts", "chan"), None),
            P(("parts", "tm", "sub"), "chan", None),
            P(),
            P(),
            P(),
            P(),
            P(),
            P("parts"),
            P("parts"),
        ),
        out_specs=P(("parts", "tm", "sub"), "chan", None),
        check_vma=False,
    )
```

```python
import jax
import jax.numpy as jnp
from jax import lax
from jax.experimental import pallas as pl
from jax.experimental.pallas import tpu as pltpu
from jax.sharding import PartitionSpec as P

ITERS = 2
TIME_AXES = ("tm", "sub")


def padded_2(block, sides, width):
    for axis, dim in sides:
        count = lax.axis_size(axis)
        forward = [(i, i + 1) for i in range(count - 1)]
        backward = [(target, source) for source, target in forward]
        low = lax.ppermute(
            lax.slice_in_dim(block, block.shape[dim] - width, None, axis=dim), axis, forward
        )
        high = lax.ppermute(lax.slice_in_dim(block, 0, width, axis=dim), axis, backward)
        block = jnp.concatenate([low, block, high], axis=dim)
    return block


def conv3x3(src_ref, w_ref, rows_out):
    steps, _, columns, channels_in = src_ref.shape
    channels_out = w_ref.shape[0]
    size = steps * rows_out * columns
    taps = []
    for col_off in range(3):
        acc = None
        for row_off in range(3):
            patch = src_ref[:, row_off : row_off + rows_out].reshape(size, channels_in)
            tap = row_off * 3 + col_off
            weight = w_ref[:, tap * channels_in : (tap + 1) * channels_in]
            part = lax.dot_general(
                patch, weight, (((1,), (1,)), ((), ())), preferred_element_type=jnp.float32
            )
            acc = part if acc is None else acc + part
        taps.append(acc)
    column = lax.broadcasted_iota(jnp.int32, (steps * rows_out, columns, channels_out), 1)
    column = column.reshape(size, channels_out)
    left = jnp.where(column == 0, 0.0, pltpu.roll(taps[0], 1, 0))
    right = jnp.where(column == columns - 1, 0.0, pltpu.roll(taps[2], size - 1, 0))
    return (left + taps[1] + right).reshape(steps, rows_out, columns, channels_out)


def silu(v):
    return v / (1.0 + jnp.exp(-v))


def row_valid(shape, first_row, total_rows):
    rows = first_row + lax.broadcasted_iota(jnp.int32, shape, 1)
    return (rows >= 0) & (rows < total_rows)


def drift_kernel(total_rows, same, first_ref, x_ref, emb_ref, w1_ref, w2_ref, w3_ref, out_ref, h1_ref, h2_ref):
    first_row = first_ref[0]
    margin = 1 if same else 0
    rows_1 = h1_ref.shape[1] - 2 * margin
    rows_2 = h2_ref.shape[1] - 2 * margin
    act = conv3x3(x_ref, w1_ref, rows_1) + emb_ref[...][:, None, None, :]
    act = jnp.where(row_valid(act.shape, first_row, total_rows), silu(act), 0.0)
    store_hidden(h1_ref, act.astype(jnp.bfloat16), margin)
    act = conv3x3(h1_ref, w2_ref, rows_2)
    act = jnp.where(row_valid(act.shape, first_row + 1 - margin, total_rows), silu(act), 0.0)
    store_hidden(h2_ref, act.astype(jnp.bfloat16), margin)
    out_ref[...] = conv3x3(h2_ref, w3_ref, out_ref.shape[1])


def store_hidden(ref, value, margin):
    if margin:
        edge = jnp.zeros((ref.shape[0], margin) + ref.shape[2:], ref.dtype)
        ref[:, :margin] = edge
        ref[:, ref.shape[1] - margin :] = edge
        ref[:, margin : ref.shape[1] - margin] = value
    else:
        ref[...] = value


def drift(x, embed, w_in, w_mid, w_out, first_row, total_rows, same):
    steps_dev, rows_in, columns, channels = x.shape
    hidden = w_in.shape[1]
    margin = 1 if same else 0
    rows_1 = rows_in - 2
    rows_2 = rows_1 + 2 * margin - 2
    rows_3 = rows_2 + 2 * margin - 2
    w1, w2, w3 = w_in.T, w_mid.T, w_out.T
    flops = 2 * steps_dev * columns * 9 * hidden * (channels * rows_1 + hidden * rows_2 + channels * rows_3)
    vmem = pl.BlockSpec(memory_space=pltpu.VMEM)
    out = pl.pallas_call(
        lambda *refs: drift_kernel(total_rows, same, *refs),
        out_shape=jax.ShapeDtypeStruct((steps_dev, rows_3, columns, channels), jnp.float32),
        in_specs=[pl.BlockSpec(memory_space=pltpu.SMEM)] + [vmem] * 5,
        out_specs=vmem,
        scratch_shapes=[
            pltpu.VMEM((steps_dev, rows_1 + 2 * margin, columns, hidden), jnp.bfloat16),
            pltpu.VMEM((steps_dev, rows_2 + 2 * margin, columns, hidden), jnp.bfloat16),
        ],
        compiler_params=pltpu.CompilerParams(vmem_limit_bytes=48 * 1024 * 1024),
        cost_estimate=pl.CostEstimate(
            flops=flops,
            transcendentals=steps_dev * columns * hidden * (rows_1 + rows_2),
            bytes_accessed=2 * (w1.size + w2.size + w3.size) + 2 * x.size + 4 * steps_dev * rows_3 * columns * channels,
        ),
    )(jnp.reshape(first_row, (1,)).astype(jnp.int32), x, embed, w1, w2, w3)
    return lax.optimization_barrier(out.reshape(steps_dev, rows_3, columns * channels))


def shifted(array, by):
    devices = lax.axis_size(TIME_AXES)
    pairs = [(i, i + by) for i in range(devices - by)]
    return lax.ppermute(array, TIME_AXES, pairs)


def scan_earlier(total, carried):
    devices = lax.axis_size(TIME_AXES)
    radix = min(devices, 8)
    earlier = None
    window = total
    moved = None
    stride = 1
    while stride < devices:
        got_all = []
        for k in range(1, radix):
            by = k * stride
            if by >= devices:
                break
            if by == 1 and carried is not None:
                both = shifted(jnp.stack([window, carried]), 1)
                got, moved = both[0], both[1]
            else:
                got = shifted(window, by)
            got_all.append(got)
        gathered = got_all[0]
        for got in got_all[1:]:
            gathered = gathered + got
        earlier = gathered if earlier is None else earlier + gathered
        stride *= radix
        if stride < devices:
            window = window + gathered
    return earlier, moved


def shards(start_state, guess, w_in, w_mid, w_out, time_embed, levels, plan, offset):
    steps_dev = guess.shape[0]
    devices = lax.axis_size(TIME_AXES)
    time_index = lax.axis_index(TIME_AXES)
    first_step = time_index * steps_dev
    positions = offset[0] + first_step + jnp.arange(steps_dev + 2, dtype=jnp.int32)
    picked = positions[:, None] == jnp.arange(plan.shape[0], dtype=jnp.int32)[None, :]
    all_ids = jnp.sum(jnp.where(picked, plan[None, :], 0), axis=1)
    one_hot = all_ids[:, None] == jnp.arange(levels.shape[0], dtype=jnp.int32)[None, :]
    noise = jnp.dot(one_hot.astype(jnp.float32), levels, precision=lax.Precision.HIGHEST)
    step_size = noise[1 : steps_dev + 1] - noise[:steps_dev]
    next_step = jnp.where(time_index < devices - 1, noise[steps_dev + 1] - noise[steps_dev], 0.0)
    embed = jnp.dot(
        one_hot[:steps_dev].astype(jnp.bfloat16), time_embed, preferred_element_type=jnp.float32
    )
    factor = jnp.where(first_step + jnp.arange(steps_dev, dtype=jnp.int32) == 0, 1.0, 1.5).astype(
        jnp.float32
    )
    channels = w_out.shape[1]
    tile_rows = guess.shape[1]
    columns = guess.shape[2] // channels
    chan = lax.axis_index("chan")
    total_rows = tile_rows * lax.axis_size("chan")
    whole_tile = lax.axis_size("chan") == 2

    def tiles(block, rows):
        return block.reshape(steps_dev, rows, columns, channels)

    step_after = jnp.concatenate([step_size[1:], next_step[None]])
    weight_on = step_size * factor - 0.5 * step_after

    def sweep_step(drift_now, carry_last):
        handed_on = jnp.sum(weight_on[:, None, None] * drift_now, axis=0)
        earlier_sum, previous = scan_earlier(handed_on, drift_now[-1] if carry_last else None)
        return drift_now, earlier_sum, previous

    def increments(drift_now):
        return [
            step_size[n] * (factor[n] * drift_now[n] - (0.5 * drift_now[n - 1] if n else 0.0))
            for n in range(steps_dev)
        ]

    def before_of(start, drift_now, earlier_sum, previous):
        increment = jnp.stack(increments(drift_now))
        running = jnp.cumsum(increment, axis=0)
        states_before = (start + earlier_sum)[None] + running - increment
        return states_before.at[0].add(0.5 * step_size[0] * previous)

    if whole_tile:
        swap = [(0, 1), (1, 0)]
        other_start = lax.ppermute(start_state, "chan", swap)
        other_guess = lax.ppermute(guess, "chan", swap)
        in_order = lambda mine, theirs, axis: jnp.where(
            chan == 0, jnp.concatenate([mine, theirs], axis=axis), jnp.concatenate([theirs, mine], axis=axis)
        )
        start_full = in_order(start_state, other_start, 0)
        layer_full = in_order(guess, other_guess, 1)
        for sweep in range(ITERS - 1):
            x = jnp.pad(tiles(layer_full, total_rows), ((0, 0), (1, 1), (0, 0), (0, 0)))
            drift_now = drift(x, embed, w_in, w_mid, w_out, jnp.int32(0), total_rows, True)
            parts = sweep_step(drift_now, True)
            layer_full = before_of(start_full, *parts).astype(jnp.bfloat16)
        padded = jnp.pad(layer_full, ((0, 0), (3, 3), (0, 0)))
        rimmed = lax.dynamic_slice_in_dim(padded, chan * tile_rows, tile_rows + 6, axis=1)
    else:
        layer_in = guess
        for sweep in range(ITERS - 1):
            rimmed = padded_2(layer_in, (("chan", 1),), 3)
            drift_now = drift(tiles(rimmed, tile_rows + 6), embed, w_in, w_mid, w_out, chan * tile_rows - 2, total_rows, False)
            parts = sweep_step(drift_now, True)
            layer_in = before_of(start_state, *parts).astype(jnp.bfloat16)
        rimmed = padded_2(layer_in, (("chan", 1),), 3)
    drift_now = drift(tiles(rimmed, tile_rows + 6), embed, w_in, w_mid, w_out, chan * tile_rows - 2, total_rows, False)
    _, earlier_sum, _ = sweep_step(drift_now, False)
    running = jnp.cumsum(jnp.stack(increments(drift_now)), axis=0)
    return (start_state + earlier_sum)[None] + running


def solution(mesh):
    return jax.shard_map(
        shards,
        mesh=mesh,
        in_specs=(
            P(("parts", "chan"), None),
            P(("parts", "tm", "sub"), "chan", None),
            P(),
            P(),
            P(),
            P(),
            P(),
            P("parts"),
            P("parts"),
        ),
        out_specs=P(("parts", "tm", "sub"), "chan", None),
        check_vma=False,
    )
```

```python
import jax
import jax.numpy as jnp
from jax import lax
from jax.experimental import pallas as pl
from jax.experimental.pallas import tpu as pltpu
from jax.sharding import PartitionSpec as P

ITERS = 2
TIME_AXES = ("tm", "sub")


def padded_2(block, sides, width):
    for axis, dim in sides:
        count = lax.axis_size(axis)
        forward = [(i, i + 1) for i in range(count - 1)]
        backward = [(target, source) for source, target in forward]
        low = lax.ppermute(
            lax.slice_in_dim(block, block.shape[dim] - width, None, axis=dim), axis, forward
        )
        high = lax.ppermute(lax.slice_in_dim(block, 0, width, axis=dim), axis, backward)
        block = jnp.concatenate([low, block, high], axis=dim)
    return block


def conv3x3(src_ref, w_ref, rows_out):
    steps, _, columns, channels_in = src_ref.shape
    channels_out = w_ref.shape[0]
    size = steps * rows_out * columns
    taps = []
    for col_off in range(3):
        acc = None
        for row_off in range(3):
            patch = src_ref[:, row_off : row_off + rows_out].reshape(size, channels_in)
            tap = row_off * 3 + col_off
            weight = w_ref[:, tap * channels_in : (tap + 1) * channels_in]
            part = lax.dot_general(
                patch, weight, (((1,), (1,)), ((), ())), preferred_element_type=jnp.float32
            )
            acc = part if acc is None else acc + part
        taps.append(acc)
    column = lax.broadcasted_iota(jnp.int32, (steps * rows_out, columns, channels_out), 1)
    column = column.reshape(size, channels_out)
    left = jnp.where(column == 0, 0.0, pltpu.roll(taps[0], 1, 0))
    right = jnp.where(column == columns - 1, 0.0, pltpu.roll(taps[2], size - 1, 0))
    return (left + taps[1] + right).reshape(steps, rows_out, columns, channels_out)


def silu(v):
    return v / (1.0 + jnp.exp(-v))


def row_valid(shape, first_row, total_rows):
    rows = first_row + lax.broadcasted_iota(jnp.int32, shape, 1)
    return (rows >= 0) & (rows < total_rows)


def drift_kernel(total_rows, same, last, first_ref, coef_ref, x_ref, emb_ref, w1_ref, w2_ref, w3_ref, states_ref, send_ref, h1_ref, h2_ref):
    first_row = first_ref[0]
    margin = 1 if same else 0
    rows_1 = h1_ref.shape[1] - 2 * margin
    rows_2 = h2_ref.shape[1] - 2 * margin
    steps = x_ref.shape[0]
    act = conv3x3(x_ref, w1_ref, rows_1) + emb_ref[...][:, None, None, :]
    act = jnp.where(row_valid(act.shape, first_row, total_rows), silu(act), 0.0)
    store_hidden(h1_ref, act.astype(jnp.bfloat16), margin)
    act = conv3x3(h1_ref, w2_ref, rows_2)
    act = jnp.where(row_valid(act.shape, first_row + 1 - margin, total_rows), silu(act), 0.0)
    store_hidden(h2_ref, act.astype(jnp.bfloat16), margin)
    drift_now = conv3x3(h2_ref, w3_ref, states_ref.shape[1])
    level = None
    handed_on = None
    for n in range(steps):
        step, factor, weight = coef_ref[n], coef_ref[steps + n], coef_ref[2 * steps + n]
        increment = step * (factor * drift_now[n] - (0.5 * drift_now[n - 1] if n else 0.0))
        if last:
            level = increment if level is None else level + increment
            states_ref[n] = level
        else:
            states_ref[n] = jnp.zeros_like(increment) if level is None else level
            level = increment if level is None else level + increment
        term = weight * drift_now[n]
        handed_on = term if handed_on is None else handed_on + term
    send_ref[0] = handed_on
    if not last:
        send_ref[1] = drift_now[steps - 1]


def store_hidden(ref, value, margin):
    if margin:
        edge = jnp.zeros((ref.shape[0], margin) + ref.shape[2:], ref.dtype)
        ref[:, :margin] = edge
        ref[:, ref.shape[1] - margin :] = edge
        ref[:, margin : ref.shape[1] - margin] = value
    else:
        ref[...] = value


def drift(x, embed, coef, w_in, w_mid, w_out, first_row, total_rows, same, last):
    steps_dev, rows_in, columns, channels = x.shape
    hidden = w_in.shape[1]
    margin = 1 if same else 0
    rows_1 = rows_in - 2
    rows_2 = rows_1 + 2 * margin - 2
    rows_3 = rows_2 + 2 * margin - 2
    w1, w2, w3 = w_in.T, w_mid.T, w_out.T
    flops = 2 * steps_dev * columns * 9 * hidden * (channels * rows_1 + hidden * rows_2 + channels * rows_3)
    vmem = pl.BlockSpec(memory_space=pltpu.VMEM)
    smem = pl.BlockSpec(memory_space=pltpu.SMEM)
    tile = (rows_3, columns, channels)
    states, send = pl.pallas_call(
        lambda *refs: drift_kernel(total_rows, same, last, *refs),
        out_shape=(
            jax.ShapeDtypeStruct((steps_dev,) + tile, jnp.float32),
            jax.ShapeDtypeStruct((1 if last else 2,) + tile, jnp.float32),
        ),
        in_specs=[smem, smem] + [vmem] * 5,
        out_specs=(vmem, vmem),
        scratch_shapes=[
            pltpu.VMEM((steps_dev, rows_1 + 2 * margin, columns, hidden), jnp.bfloat16),
            pltpu.VMEM((steps_dev, rows_2 + 2 * margin, columns, hidden), jnp.bfloat16),
        ],
        compiler_params=pltpu.CompilerParams(vmem_limit_bytes=48 * 1024 * 1024),
        cost_estimate=pl.CostEstimate(
            flops=flops,
            transcendentals=steps_dev * columns * hidden * (rows_1 + rows_2),
            bytes_accessed=2 * (w1.size + w2.size + w3.size) + 2 * x.size + 4 * (steps_dev + 2) * rows_3 * columns * channels,
        ),
    )(jnp.reshape(first_row, (1,)).astype(jnp.int32), coef, x, embed, w1, w2, w3)
    return states, lax.optimization_barrier(send.reshape(send.shape[0], rows_3, columns * channels))


def shifted(array, by):
    devices = lax.axis_size(TIME_AXES)
    pairs = [(i, i + by) for i in range(devices - by)]
    return lax.ppermute(array, TIME_AXES, pairs)


def scan_earlier(total, carried):
    devices = lax.axis_size(TIME_AXES)
    radix = min(devices, 8)
    earlier = None
    window = total
    moved = None
    stride = 1
    while stride < devices:
        got_all = []
        for k in range(1, radix):
            by = k * stride
            if by >= devices:
                break
            if by == 1 and carried is not None:
                both = shifted(jnp.stack([window, carried]), 1)
                got, moved = both[0], both[1]
            else:
                got = shifted(window, by)
            got_all.append(got)
        gathered = got_all[0]
        for got in got_all[1:]:
            gathered = gathered + got
        earlier = gathered if earlier is None else earlier + gathered
        stride *= radix
        if stride < devices:
            window = window + gathered
    return earlier, moved


def shards(start_state, guess, w_in, w_mid, w_out, time_embed, levels, plan, offset):
    steps_dev = guess.shape[0]
    devices = lax.axis_size(TIME_AXES)
    time_index = lax.axis_index(TIME_AXES)
    first_step = time_index * steps_dev
    positions = offset[0] + first_step + jnp.arange(steps_dev + 2, dtype=jnp.int32)
    picked = positions[:, None] == jnp.arange(plan.shape[0], dtype=jnp.int32)[None, :]
    all_ids = jnp.sum(jnp.where(picked, plan[None, :], 0), axis=1)
    one_hot = all_ids[:, None] == jnp.arange(levels.shape[0], dtype=jnp.int32)[None, :]
    noise = jnp.dot(one_hot.astype(jnp.float32), levels, precision=lax.Precision.HIGHEST)
    step_size = noise[1 : steps_dev + 1] - noise[:steps_dev]
    next_step = jnp.where(time_index < devices - 1, noise[steps_dev + 1] - noise[steps_dev], 0.0)
    embed = jnp.dot(
        one_hot[:steps_dev].astype(jnp.bfloat16), time_embed, preferred_element_type=jnp.float32
    )
    factor = jnp.where(first_step + jnp.arange(steps_dev, dtype=jnp.int32) == 0, 1.0, 1.5).astype(
        jnp.float32
    )
    channels = w_out.shape[1]
    tile_rows = guess.shape[1]
    columns = guess.shape[2] // channels
    chan = lax.axis_index("chan")
    total_rows = tile_rows * lax.axis_size("chan")
    whole_tile = lax.axis_size("chan") == 2
    step_after = jnp.concatenate([step_size[1:], next_step[None]])
    coef = jnp.concatenate([step_size, factor, step_size * factor - 0.5 * step_after])

    def tiles(block):
        return block.reshape(block.shape[:-1] + (columns, channels))

    def sweep(x, first_row, same, last):
        states, send = drift(x, embed, coef, w_in, w_mid, w_out, first_row, total_rows, same, last)
        earlier_sum, previous = scan_earlier(send[0], None if last else send[1])
        return states, earlier_sum, previous

    def before_of(start, states, earlier_sum, previous):
        level = tiles(start + earlier_sum)
        first = tiles(0.5 * step_size[0] * previous)
        return (level[None] + states).at[0].add(first).astype(jnp.bfloat16)

    if whole_tile:
        own = jnp.concatenate([start_state[None], guess.astype(jnp.float32)], axis=0)
        other = lax.ppermute(own, "chan", [(0, 1), (1, 0)])
        full = jnp.where(chan == 0, jnp.concatenate([own, other], axis=1), jnp.concatenate([other, own], axis=1))
        start_full = full[0]
        layer_full = tiles(full[1:].astype(jnp.bfloat16))
        for _ in range(ITERS - 1):
            x = jnp.pad(layer_full, ((0, 0), (1, 1), (0, 0), (0, 0)))
            parts = sweep(x, jnp.int32(0), True, False)
            layer_full = before_of(start_full, *parts)
        padded = jnp.pad(layer_full, ((0, 0), (3, 3), (0, 0), (0, 0)))
        rimmed = lax.dynamic_slice_in_dim(padded, chan * tile_rows, tile_rows + 6, axis=1)
    else:
        layer_in = tiles(guess)
        for _ in range(ITERS - 1):
            rimmed = padded_2(layer_in, (("chan", 1),), 3)
            parts = sweep(rimmed, chan * tile_rows - 2, False, False)
            layer_in = before_of(start_state, *parts)
        rimmed = padded_2(layer_in, (("chan", 1),), 3)
    states, earlier_sum, _ = sweep(rimmed, chan * tile_rows - 2, False, True)
    states_after = tiles(start_state + earlier_sum)[None] + states
    return states_after.reshape(guess.shape)


def solution(mesh):
    return jax.shard_map(
        shards,
        mesh=mesh,
        in_specs=(
            P(("parts", "chan"), None),
            P(("parts", "tm", "sub"), "chan", None),
            P(),
            P(),
            P(),
            P(),
            P(),
            P("parts"),
            P("parts"),
        ),
        out_specs=P(("parts", "tm", "sub"), "chan", None),
        check_vma=False,
    )
```

```python
import jax
import jax.numpy as jnp
from jax import lax
from jax.experimental import pallas as pl
from jax.experimental.pallas import tpu as pltpu
from jax.sharding import PartitionSpec as P

ITERS = 2
TIME_AXES = ("tm", "sub")


def padded_2(block, sides, width):
    for axis, dim in sides:
        count = lax.axis_size(axis)
        forward = [(i, i + 1) for i in range(count - 1)]
        backward = [(target, source) for source, target in forward]
        low = lax.ppermute(
            lax.slice_in_dim(block, block.shape[dim] - width, None, axis=dim), axis, forward
        )
        high = lax.ppermute(lax.slice_in_dim(block, 0, width, axis=dim), axis, backward)
        block = jnp.concatenate([low, block, high], axis=dim)
    return block


def conv3x3(src_ref, w_ref, rows_out):
    steps, _, columns, channels_in = src_ref.shape
    channels_out = w_ref.shape[0]
    size = steps * rows_out * columns
    taps = []
    for col_off in range(3):
        acc = None
        for row_off in range(3):
            patch = src_ref[:, row_off : row_off + rows_out].reshape(size, channels_in)
            tap = row_off * 3 + col_off
            weight = w_ref[:, tap * channels_in : (tap + 1) * channels_in]
            part = lax.dot_general(
                patch, weight, (((1,), (1,)), ((), ())), preferred_element_type=jnp.float32
            )
            acc = part if acc is None else acc + part
        taps.append(acc)
    column = lax.broadcasted_iota(jnp.int32, (steps * rows_out, columns, channels_out), 1)
    column = column.reshape(size, channels_out)
    left = jnp.where(column == 0, 0.0, pltpu.roll(taps[0], 1, 0))
    right = jnp.where(column == columns - 1, 0.0, pltpu.roll(taps[2], size - 1, 0))
    return (left + taps[1] + right).reshape(steps, rows_out, columns, channels_out)


def silu(v):
    return v / (1.0 + jnp.exp(-v))


def row_valid(shape, first_row, total_rows):
    rows = first_row + lax.broadcasted_iota(jnp.int32, shape, 1)
    return (rows >= 0) & (rows < total_rows)


def drift_kernel(
    total_rows, same, last, first_ref, coef_ref, x_ref, emb_ref, w1_hbm, w2_hbm, w3_hbm,
    states_ref, send_ref, h1_ref, h2_ref, w1_ref, w2_ref, w3_ref, sems,
):
    copies = [
        pltpu.make_async_copy(src, dst, sems.at[k])
        for k, (src, dst) in enumerate(((w1_hbm, w1_ref), (w2_hbm, w2_ref), (w3_hbm, w3_ref)))
    ]
    for copy in copies:
        copy.start()
    first_row = first_ref[0]
    margin = 1 if same else 0
    rows_1 = h1_ref.shape[1] - 2 * margin
    rows_2 = h2_ref.shape[1] - 2 * margin
    steps = x_ref.shape[0]
    copies[0].wait()
    act = conv3x3(x_ref, w1_ref, rows_1) + emb_ref[...][:, None, None, :]
    act = jnp.where(row_valid(act.shape, first_row, total_rows), silu(act), 0.0)
    store_hidden(h1_ref, act.astype(jnp.bfloat16), margin)
    copies[1].wait()
    act = conv3x3(h1_ref, w2_ref, rows_2)
    act = jnp.where(row_valid(act.shape, first_row + 1 - margin, total_rows), silu(act), 0.0)
    store_hidden(h2_ref, act.astype(jnp.bfloat16), margin)
    copies[2].wait()
    drift_now = conv3x3(h2_ref, w3_ref, states_ref.shape[1])
    level = None
    handed_on = None
    for n in range(steps):
        step, factor, weight = coef_ref[n], coef_ref[steps + n], coef_ref[2 * steps + n]
        increment = step * (factor * drift_now[n] - (0.5 * drift_now[n - 1] if n else 0.0))
        if last:
            level = increment if level is None else level + increment
            states_ref[n] = level
        else:
            states_ref[n] = jnp.zeros_like(increment) if level is None else level
            level = increment if level is None else level + increment
        term = weight * drift_now[n]
        handed_on = term if handed_on is None else handed_on + term
    send_ref[0] = handed_on
    if not last:
        send_ref[1] = drift_now[steps - 1]


def store_hidden(ref, value, margin):
    if margin:
        edge = jnp.zeros((ref.shape[0], margin) + ref.shape[2:], ref.dtype)
        ref[:, :margin] = edge
        ref[:, ref.shape[1] - margin :] = edge
        ref[:, margin : ref.shape[1] - margin] = value
    else:
        ref[...] = value


def drift(x, embed, coef, w_in, w_mid, w_out, first_row, total_rows, same, last):
    steps_dev, rows_in, columns, channels = x.shape
    hidden = w_in.shape[1]
    margin = 1 if same else 0
    rows_1 = rows_in - 2
    rows_2 = rows_1 + 2 * margin - 2
    rows_3 = rows_2 + 2 * margin - 2
    w1, w2, w3 = w_in.T, w_mid.T, w_out.T
    flops = 2 * steps_dev * columns * 9 * hidden * (channels * rows_1 + hidden * rows_2 + channels * rows_3)
    vmem = pl.BlockSpec(memory_space=pltpu.VMEM)
    smem = pl.BlockSpec(memory_space=pltpu.SMEM)
    tile = (rows_3, columns, channels)
    states, send = pl.pallas_call(
        lambda *refs: drift_kernel(total_rows, same, last, *refs),
        out_shape=(
            jax.ShapeDtypeStruct((steps_dev,) + tile, jnp.float32),
            jax.ShapeDtypeStruct((1 if last else 2,) + tile, jnp.float32),
        ),
        in_specs=[smem, smem, vmem, vmem] + [pl.BlockSpec(memory_space=pl.ANY)] * 3,
        out_specs=(vmem, vmem),
        scratch_shapes=[
            pltpu.VMEM((steps_dev, rows_1 + 2 * margin, columns, hidden), jnp.bfloat16),
            pltpu.VMEM((steps_dev, rows_2 + 2 * margin, columns, hidden), jnp.bfloat16),
            pltpu.VMEM(w1.shape, w1.dtype),
            pltpu.VMEM(w2.shape, w2.dtype),
            pltpu.VMEM(w3.shape, w3.dtype),
            pltpu.SemaphoreType.DMA((3,)),
        ],
        compiler_params=pltpu.CompilerParams(vmem_limit_bytes=64 * 1024 * 1024 - 65536),
        cost_estimate=pl.CostEstimate(
            flops=flops,
            transcendentals=steps_dev * columns * hidden * (rows_1 + rows_2),
            bytes_accessed=2 * (w1.size + w2.size + w3.size) + 2 * x.size + 4 * (steps_dev + 2) * rows_3 * columns * channels,
        ),
    )(jnp.reshape(first_row, (1,)).astype(jnp.int32), coef, x, embed, w1, w2, w3)
    return states, lax.optimization_barrier(send.reshape(send.shape[0], rows_3, columns * channels))


def shifted(array, by):
    devices = lax.axis_size(TIME_AXES)
    pairs = [(i, i + by) for i in range(devices - by)]
    return lax.ppermute(array, TIME_AXES, pairs)


def scan_earlier(total, carried):
    devices = lax.axis_size(TIME_AXES)
    radix = min(devices, 8)
    earlier = None
    window = total
    moved = None
    stride = 1
    while stride < devices:
        got_all = []
        for k in range(1, radix):
            by = k * stride
            if by >= devices:
                break
            if by == 1 and carried is not None:
                both = shifted(jnp.stack([window, carried]), 1)
                got, moved = both[0], both[1]
            else:
                got = shifted(window, by)
            got_all.append(got)
        gathered = got_all[0]
        for got in got_all[1:]:
            gathered = gathered + got
        earlier = gathered if earlier is None else earlier + gathered
        stride *= radix
        if stride < devices:
            window = window + gathered
    return earlier, moved


def shards(start_state, guess, w_in, w_mid, w_out, time_embed, levels, plan, offset):
    steps_dev = guess.shape[0]
    devices = lax.axis_size(TIME_AXES)
    time_index = lax.axis_index(TIME_AXES)
    first_step = time_index * steps_dev
    positions = offset[0] + first_step + jnp.arange(steps_dev + 2, dtype=jnp.int32)
    picked = positions[:, None] == jnp.arange(plan.shape[0], dtype=jnp.int32)[None, :]
    all_ids = jnp.sum(jnp.where(picked, plan[None, :], 0), axis=1)
    one_hot = all_ids[:, None] == jnp.arange(levels.shape[0], dtype=jnp.int32)[None, :]
    noise = jnp.dot(one_hot.astype(jnp.float32), levels, precision=lax.Precision.HIGHEST)
    step_size = noise[1 : steps_dev + 1] - noise[:steps_dev]
    next_step = jnp.where(time_index < devices - 1, noise[steps_dev + 1] - noise[steps_dev], 0.0)
    embed = jnp.dot(
        one_hot[:steps_dev].astype(jnp.bfloat16), time_embed, preferred_element_type=jnp.float32
    )
    factor = jnp.where(first_step + jnp.arange(steps_dev, dtype=jnp.int32) == 0, 1.0, 1.5).astype(
        jnp.float32
    )
    channels = w_out.shape[1]
    tile_rows = guess.shape[1]
    columns = guess.shape[2] // channels
    chan = lax.axis_index("chan")
    total_rows = tile_rows * lax.axis_size("chan")
    whole_tile = lax.axis_size("chan") == 2
    step_after = jnp.concatenate([step_size[1:], next_step[None]])
    coef = jnp.concatenate([step_size, factor, step_size * factor - 0.5 * step_after])

    def tiles(block):
        return block.reshape(block.shape[:-1] + (columns, channels))

    def sweep(x, first_row, same, last):
        states, send = drift(x, embed, coef, w_in, w_mid, w_out, first_row, total_rows, same, last)
        earlier_sum, previous = scan_earlier(send[0], None if last else send[1])
        return states, earlier_sum, previous

    def before_of(start, states, earlier_sum, previous):
        level = tiles(start + earlier_sum)
        first = tiles(0.5 * step_size[0] * previous)
        return (level[None] + states).at[0].add(first).astype(jnp.bfloat16)

    if whole_tile:
        own = jnp.concatenate([start_state[None], guess.astype(jnp.float32)], axis=0)
        other = lax.ppermute(own, "chan", [(0, 1), (1, 0)])
        full = jnp.where(chan == 0, jnp.concatenate([own, other], axis=1), jnp.concatenate([other, own], axis=1))
        start_full = full[0]
        layer_full = tiles(full[1:].astype(jnp.bfloat16))
        for _ in range(ITERS - 1):
            x = jnp.pad(layer_full, ((0, 0), (1, 1), (0, 0), (0, 0)))
            parts = sweep(x, jnp.int32(0), True, False)
            layer_full = before_of(start_full, *parts)
        padded = jnp.pad(layer_full, ((0, 0), (3, 3), (0, 0), (0, 0)))
        rimmed = lax.dynamic_slice_in_dim(padded, chan * tile_rows, tile_rows + 6, axis=1)
    else:
        layer_in = tiles(guess)
        for _ in range(ITERS - 1):
            rimmed = padded_2(layer_in, (("chan", 1),), 3)
            parts = sweep(rimmed, chan * tile_rows - 2, False, False)
            layer_in = before_of(start_state, *parts)
        rimmed = padded_2(layer_in, (("chan", 1),), 3)
    states, earlier_sum, _ = sweep(rimmed, chan * tile_rows - 2, False, True)
    states_after = tiles(start_state + earlier_sum)[None] + states
    return states_after.reshape(guess.shape)


def solution(mesh):
    return jax.shard_map(
        shards,
        mesh=mesh,
        in_specs=(
            P(("parts", "chan"), None),
            P(("parts", "tm", "sub"), "chan", None),
            P(),
            P(),
            P(),
            P(),
            P(),
            P("parts"),
            P("parts"),
        ),
        out_specs=P(("parts", "tm", "sub"), "chan", None),
        check_vma=False,
    )
```

```python
import jax
import jax.numpy as jnp
from jax import lax
from jax.experimental import pallas as pl
from jax.experimental.pallas import tpu as pltpu
from jax.sharding import PartitionSpec as P

ITERS = 2
TIME_AXES = ("tm", "sub")


def padded_2(block, sides, width):
    for axis, dim in sides:
        count = lax.axis_size(axis)
        forward = [(i, i + 1) for i in range(count - 1)]
        backward = [(target, source) for source, target in forward]
        low = lax.ppermute(
            lax.slice_in_dim(block, block.shape[dim] - width, None, axis=dim), axis, forward
        )
        high = lax.ppermute(lax.slice_in_dim(block, 0, width, axis=dim), axis, backward)
        block = jnp.concatenate([low, block, high], axis=dim)
    return block


def conv3x3(src_ref, w_ref, rows_out):
    steps, _, columns, channels_in = src_ref.shape
    channels_out = w_ref.shape[0]
    size = steps * rows_out * columns
    taps = []
    for col_off in range(3):
        acc = None
        for row_off in range(3):
            patch = src_ref[:, row_off : row_off + rows_out].reshape(size, channels_in)
            tap = row_off * 3 + col_off
            weight = w_ref[:, tap * channels_in : (tap + 1) * channels_in]
            part = lax.dot_general(
                patch, weight, (((1,), (1,)), ((), ())), preferred_element_type=jnp.float32
            )
            acc = part if acc is None else acc + part
        taps.append(acc)
    column = lax.broadcasted_iota(jnp.int32, (steps * rows_out, columns, channels_out), 1)
    column = column.reshape(size, channels_out)
    left = jnp.where(column == 0, 0.0, pltpu.roll(taps[0], 1, 0))
    right = jnp.where(column == columns - 1, 0.0, pltpu.roll(taps[2], size - 1, 0))
    return (left + taps[1] + right).reshape(steps, rows_out, columns, channels_out)


def silu(v):
    return v / (1.0 + jnp.exp(-v))


def row_valid(shape, first_row, total_rows):
    rows = first_row + lax.broadcasted_iota(jnp.int32, shape, 1)
    return (rows >= 0) & (rows < total_rows)


def drift_kernel(total_rows, same, last, first_ref, coef_ref, x_ref, emb_ref, w1_ref, w2_ref, w3_ref, states_ref, send_ref, h1_ref, h2_ref):
    first_row = first_ref[0]
    margin = 1 if same else 0
    rows_1 = h1_ref.shape[1] - 2 * margin
    rows_2 = h2_ref.shape[1] - 2 * margin
    steps = x_ref.shape[0]
    act = conv3x3(x_ref, w1_ref, rows_1) + emb_ref[...][:, None, None, :]
    act = jnp.where(row_valid(act.shape, first_row, total_rows), silu(act), 0.0)
    store_hidden(h1_ref, act.astype(jnp.bfloat16), margin)
    act = conv3x3(h1_ref, w2_ref, rows_2)
    act = jnp.where(row_valid(act.shape, first_row + 1 - margin, total_rows), silu(act), 0.0)
    store_hidden(h2_ref, act.astype(jnp.bfloat16), margin)
    drift_now = conv3x3(h2_ref, w3_ref, states_ref.shape[1])
    level = None
    handed_on = None
    for n in range(steps):
        step, factor, weight = coef_ref[n], coef_ref[steps + n], coef_ref[2 * steps + n]
        increment = step * (factor * drift_now[n] - (0.5 * drift_now[n - 1] if n else 0.0))
        if last:
            level = increment if level is None else level + increment
            states_ref[n] = level
        else:
            states_ref[n] = jnp.zeros_like(increment) if level is None else level
            level = increment if level is None else level + increment
        term = weight * drift_now[n]
        handed_on = term if handed_on is None else handed_on + term
    send_ref[0] = handed_on
    if not last:
        send_ref[1] = drift_now[steps - 1]


def store_hidden(ref, value, margin):
    if margin:
        edge = jnp.zeros((ref.shape[0], margin) + ref.shape[2:], ref.dtype)
        ref[:, :margin] = edge
        ref[:, ref.shape[1] - margin :] = edge
        ref[:, margin : ref.shape[1] - margin] = value
    else:
        ref[...] = value


def drift(x, embed, coef, w_in, w_mid, w_out, first_row, total_rows, same, last):
    steps_dev, rows_in, columns, channels = x.shape
    hidden = w_in.shape[1]
    margin = 1 if same else 0
    rows_1 = rows_in - 2
    rows_2 = rows_1 + 2 * margin - 2
    rows_3 = rows_2 + 2 * margin - 2
    w1, w2, w3 = w_in.T, w_mid.T, w_out.T
    flops = 2 * steps_dev * columns * 9 * hidden * (channels * rows_1 + hidden * rows_2 + channels * rows_3)
    vmem = pl.BlockSpec(memory_space=pltpu.VMEM)
    smem = pl.BlockSpec(memory_space=pltpu.SMEM)
    tile = (rows_3, columns, channels)
    states, send = pl.pallas_call(
        lambda *refs: drift_kernel(total_rows, same, last, *refs),
        out_shape=(
            jax.ShapeDtypeStruct((steps_dev,) + tile, jnp.float32),
            jax.ShapeDtypeStruct((1 if last else 2,) + tile, jnp.float32),
        ),
        in_specs=[smem, smem] + [vmem] * 5,
        out_specs=(vmem, vmem),
        scratch_shapes=[
            pltpu.VMEM((steps_dev, rows_1 + 2 * margin, columns, hidden), jnp.bfloat16),
            pltpu.VMEM((steps_dev, rows_2 + 2 * margin, columns, hidden), jnp.bfloat16),
        ],
        compiler_params=pltpu.CompilerParams(vmem_limit_bytes=48 * 1024 * 1024),
        cost_estimate=pl.CostEstimate(
            flops=flops,
            transcendentals=steps_dev * columns * hidden * (rows_1 + rows_2),
            bytes_accessed=2 * (w1.size + w2.size + w3.size) + 2 * x.size + 4 * (steps_dev + 2) * rows_3 * columns * channels,
        ),
    )(jnp.reshape(first_row, (1,)).astype(jnp.int32), coef, x, embed, w1, w2, w3)
    return states, lax.optimization_barrier(send.reshape(send.shape[0], rows_3, columns * channels))


def shifted(array, by):
    devices = lax.axis_size(TIME_AXES)
    pairs = [(i, i + by) for i in range(devices - by)]
    return lax.ppermute(array, TIME_AXES, pairs)


def scan_earlier(total, carried):
    devices = lax.axis_size(TIME_AXES)
    earlier = None
    window = total
    moved = None
    stride = 1
    while stride < devices:
        radix = 2 if stride == 1 else 8
        got_all = []
        for k in range(1, radix):
            by = k * stride
            if by >= devices:
                break
            if by == 1 and carried is not None:
                both = shifted(jnp.stack([window, carried]), 1)
                got, moved = both[0], both[1]
            else:
                got = shifted(window, by)
            got_all.append(got)
        gathered = got_all[0]
        for got in got_all[1:]:
            gathered = gathered + got
        earlier = gathered if earlier is None else earlier + gathered
        stride *= radix
        if stride < devices:
            window = window + gathered
    return earlier, moved


def shards(start_state, guess, w_in, w_mid, w_out, time_embed, levels, plan, offset):
    steps_dev = guess.shape[0]
    devices = lax.axis_size(TIME_AXES)
    time_index = lax.axis_index(TIME_AXES)
    first_step = time_index * steps_dev
    positions = offset[0] + first_step + jnp.arange(steps_dev + 2, dtype=jnp.int32)
    picked = positions[:, None] == jnp.arange(plan.shape[0], dtype=jnp.int32)[None, :]
    all_ids = jnp.sum(jnp.where(picked, plan[None, :], 0), axis=1)
    one_hot = all_ids[:, None] == jnp.arange(levels.shape[0], dtype=jnp.int32)[None, :]
    noise = jnp.dot(one_hot.astype(jnp.float32), levels, precision=lax.Precision.HIGHEST)
    step_size = noise[1 : steps_dev + 1] - noise[:steps_dev]
    next_step = jnp.where(time_index < devices - 1, noise[steps_dev + 1] - noise[steps_dev], 0.0)
    embed = jnp.dot(
        one_hot[:steps_dev].astype(jnp.bfloat16), time_embed, preferred_element_type=jnp.float32
    )
    factor = jnp.where(first_step + jnp.arange(steps_dev, dtype=jnp.int32) == 0, 1.0, 1.5).astype(
        jnp.float32
    )
    channels = w_out.shape[1]
    tile_rows = guess.shape[1]
    columns = guess.shape[2] // channels
    chan = lax.axis_index("chan")
    total_rows = tile_rows * lax.axis_size("chan")
    whole_tile = lax.axis_size("chan") == 2
    step_after = jnp.concatenate([step_size[1:], next_step[None]])
    coef = jnp.concatenate([step_size, factor, step_size * factor - 0.5 * step_after])

    def tiles(block):
        return block.reshape(block.shape[:-1] + (columns, channels))

    def sweep(x, first_row, same, last):
        states, send = drift(x, embed, coef, w_in, w_mid, w_out, first_row, total_rows, same, last)
        earlier_sum, previous = scan_earlier(send[0], None if last else send[1])
        return states, earlier_sum, previous

    def before_of(start, states, earlier_sum, previous):
        level = tiles(start + earlier_sum)
        first = tiles(0.5 * step_size[0] * previous)
        return (level[None] + states).at[0].add(first).astype(jnp.bfloat16)

    if whole_tile:
        own = jnp.concatenate([start_state[None], guess.astype(jnp.float32)], axis=0)
        other = lax.ppermute(own, "chan", [(0, 1), (1, 0)])
        full = jnp.where(chan == 0, jnp.concatenate([own, other], axis=1), jnp.concatenate([other, own], axis=1))
        start_full = full[0]
        layer_full = tiles(full[1:].astype(jnp.bfloat16))
        for _ in range(ITERS - 1):
            x = jnp.pad(layer_full, ((0, 0), (1, 1), (0, 0), (0, 0)))
            parts = sweep(x, jnp.int32(0), True, False)
            layer_full = before_of(start_full, *parts)
        padded = jnp.pad(layer_full, ((0, 0), (3, 3), (0, 0), (0, 0)))
        rimmed = lax.dynamic_slice_in_dim(padded, chan * tile_rows, tile_rows + 6, axis=1)
    else:
        layer_in = tiles(guess)
        for _ in range(ITERS - 1):
            rimmed = padded_2(layer_in, (("chan", 1),), 3)
            parts = sweep(rimmed, chan * tile_rows - 2, False, False)
            layer_in = before_of(start_state, *parts)
        rimmed = padded_2(layer_in, (("chan", 1),), 3)
    states, earlier_sum, _ = sweep(rimmed, chan * tile_rows - 2, False, True)
    states_after = tiles(start_state + earlier_sum)[None] + states
    return states_after.reshape(guess.shape)


def solution(mesh):
    return jax.shard_map(
        shards,
        mesh=mesh,
        in_specs=(
            P(("parts", "chan"), None),
            P(("parts", "tm", "sub"), "chan", None),
            P(),
            P(),
            P(),
            P(),
            P(),
            P("parts"),
            P("parts"),
        ),
        out_specs=P(("parts", "tm", "sub"), "chan", None),
        check_vma=False,
    )
```

```python
import jax
import jax.numpy as jnp
from jax import lax
from jax.experimental import pallas as pl
from jax.experimental.pallas import tpu as pltpu
from jax.sharding import PartitionSpec as P

ITERS = 2
TIME_AXES = ("tm", "sub")


def padded_2(block, sides, width):
    for axis, dim in sides:
        count = lax.axis_size(axis)
        forward = [(i, i + 1) for i in range(count - 1)]
        backward = [(target, source) for source, target in forward]
        low = lax.ppermute(
            lax.slice_in_dim(block, block.shape[dim] - width, None, axis=dim), axis, forward
        )
        high = lax.ppermute(lax.slice_in_dim(block, 0, width, axis=dim), axis, backward)
        block = jnp.concatenate([low, block, high], axis=dim)
    return block


def conv3x3(src_ref, w_ref, rows_out):
    steps, _, columns, channels_in = src_ref.shape
    channels_out = w_ref.shape[0]
    size = steps * rows_out * columns
    taps = []
    for col_off in range(3):
        acc = None
        for row_off in range(3):
            patch = src_ref[:, row_off : row_off + rows_out].reshape(size, channels_in)
            tap = row_off * 3 + col_off
            weight = w_ref[:, tap * channels_in : (tap + 1) * channels_in]
            part = lax.dot_general(
                patch, weight, (((1,), (1,)), ((), ())), preferred_element_type=jnp.float32
            )
            acc = part if acc is None else acc + part
        taps.append(acc)
    column = lax.broadcasted_iota(jnp.int32, (steps * rows_out, columns, channels_out), 1)
    column = column.reshape(size, channels_out)
    left = jnp.where(column == 0, 0.0, pltpu.roll(taps[0], 1, 0))
    right = jnp.where(column == columns - 1, 0.0, pltpu.roll(taps[2], size - 1, 0))
    return (left + taps[1] + right).reshape(steps, rows_out, columns, channels_out)


def silu(v):
    return v / (1.0 + jnp.exp(-v))


def row_valid(shape, first_row, total_rows):
    rows = first_row + lax.broadcasted_iota(jnp.int32, shape, 1)
    return (rows >= 0) & (rows < total_rows)


def drift_kernel(total_rows, same, last, first_ref, coef_ref, x_ref, emb_ref, w1_ref, w2_ref, w3_ref, states_ref, send_ref, h1_ref, h2_ref):
    first_row = first_ref[0]
    margin = 1 if same else 0
    rows_1 = h1_ref.shape[1] - 2 * margin
    rows_2 = h2_ref.shape[1] - 2 * margin
    steps = x_ref.shape[0]
    act = conv3x3(x_ref, w1_ref, rows_1) + emb_ref[...][:, None, None, :]
    act = jnp.where(row_valid(act.shape, first_row, total_rows), silu(act), 0.0)
    store_hidden(h1_ref, act.astype(jnp.bfloat16), margin)
    act = conv3x3(h1_ref, w2_ref, rows_2)
    act = jnp.where(row_valid(act.shape, first_row + 1 - margin, total_rows), silu(act), 0.0)
    store_hidden(h2_ref, act.astype(jnp.bfloat16), margin)
    drift_now = conv3x3(h2_ref, w3_ref, states_ref.shape[1])
    level = None
    handed_on = None
    for n in range(steps):
        step, factor, weight = coef_ref[n], coef_ref[steps + n], coef_ref[2 * steps + n]
        increment = step * (factor * drift_now[n] - (0.5 * drift_now[n - 1] if n else 0.0))
        if last:
            level = increment if level is None else level + increment
            states_ref[n] = level
        else:
            states_ref[n] = jnp.zeros_like(increment) if level is None else level
            level = increment if level is None else level + increment
        term = weight * drift_now[n]
        handed_on = term if handed_on is None else handed_on + term
    send_ref[0] = handed_on
    if not last:
        send_ref[1] = drift_now[steps - 1]


def store_hidden(ref, value, margin):
    if margin:
        edge = jnp.zeros((ref.shape[0], margin) + ref.shape[2:], ref.dtype)
        ref[:, :margin] = edge
        ref[:, ref.shape[1] - margin :] = edge
        ref[:, margin : ref.shape[1] - margin] = value
    else:
        ref[...] = value


def drift(x, embed, coef, w_in, w_mid, w_out, first_row, total_rows, same, last):
    steps_dev, rows_in, columns, channels = x.shape
    hidden = w_in.shape[1]
    margin = 1 if same else 0
    rows_1 = rows_in - 2
    rows_2 = rows_1 + 2 * margin - 2
    rows_3 = rows_2 + 2 * margin - 2
    w1, w2, w3 = w_in.T, w_mid.T, w_out.T
    flops = 2 * steps_dev * columns * 9 * hidden * (channels * rows_1 + hidden * rows_2 + channels * rows_3)
    vmem = pl.BlockSpec(memory_space=pltpu.VMEM)
    smem = pl.BlockSpec(memory_space=pltpu.SMEM)
    tile = (rows_3, columns, channels)
    states, send = pl.pallas_call(
        lambda *refs: drift_kernel(total_rows, same, last, *refs),
        out_shape=(
            jax.ShapeDtypeStruct((steps_dev,) + tile, jnp.float32),
            jax.ShapeDtypeStruct((1 if last else 2,) + tile, jnp.float32),
        ),
        in_specs=[smem, smem] + [vmem] * 5,
        out_specs=(vmem, vmem),
        scratch_shapes=[
            pltpu.VMEM((steps_dev, rows_1 + 2 * margin, columns, hidden), jnp.bfloat16),
            pltpu.VMEM((steps_dev, rows_2 + 2 * margin, columns, hidden), jnp.bfloat16),
        ],
        compiler_params=pltpu.CompilerParams(vmem_limit_bytes=48 * 1024 * 1024),
        cost_estimate=pl.CostEstimate(
            flops=flops,
            transcendentals=steps_dev * columns * hidden * (rows_1 + rows_2),
            bytes_accessed=2 * (w1.size + w2.size + w3.size) + 2 * x.size + 4 * (steps_dev + 2) * rows_3 * columns * channels,
        ),
    )(jnp.reshape(first_row, (1,)).astype(jnp.int32), coef, x, embed, w1, w2, w3)
    return states, lax.optimization_barrier(send.reshape(send.shape[0], rows_3, columns * channels))


def shifted(array, by):
    devices = lax.axis_size(TIME_AXES)
    pairs = [(i, i + by) for i in range(devices - by)]
    return lax.ppermute(array, TIME_AXES, pairs)


def scan_earlier(total, carried):
    devices = lax.axis_size(TIME_AXES)
    earlier = None
    window = total
    moved = None
    stride = 1
    while stride < devices:
        radix = 2 if stride == 1 else 8
        got_all = []
        for k in range(1, radix):
            by = k * stride
            if by >= devices:
                break
            if by == 1 and carried is not None:
                both = shifted(jnp.stack([window, carried]), 1)
                got, moved = both[0], both[1]
            else:
                got = shifted(window, by)
            got_all.append(got)
        gathered = got_all[0]
        for got in got_all[1:]:
            gathered = gathered + got
        earlier = gathered if earlier is None else earlier + gathered
        stride *= radix
        if stride < devices:
            window = window + gathered
    return earlier, moved


def shards(start_state, guess, w_in, w_mid, w_out, time_embed, levels, plan, offset):
    steps_dev = guess.shape[0]
    devices = lax.axis_size(TIME_AXES)
    time_index = lax.axis_index(TIME_AXES)
    first_step = time_index * steps_dev
    positions = offset[0] + first_step + jnp.arange(steps_dev + 2, dtype=jnp.int32)
    picked = positions[:, None] == jnp.arange(plan.shape[0], dtype=jnp.int32)[None, :]
    all_ids = jnp.sum(jnp.where(picked, plan[None, :], 0), axis=1)
    one_hot = all_ids[:, None] == jnp.arange(levels.shape[0], dtype=jnp.int32)[None, :]
    noise = jnp.dot(one_hot.astype(jnp.float32), levels, precision=lax.Precision.HIGHEST)
    step_size = noise[1 : steps_dev + 1] - noise[:steps_dev]
    next_step = jnp.where(time_index < devices - 1, noise[steps_dev + 1] - noise[steps_dev], 0.0)
    embed = jnp.dot(
        one_hot[:steps_dev].astype(jnp.bfloat16), time_embed, preferred_element_type=jnp.float32
    )
    factor = jnp.where(first_step + jnp.arange(steps_dev, dtype=jnp.int32) == 0, 1.0, 1.5).astype(
        jnp.float32
    )
    channels = w_out.shape[1]
    tile_rows = guess.shape[1]
    columns = guess.shape[2] // channels
    chan = lax.axis_index("chan")
    total_rows = tile_rows * lax.axis_size("chan")
    whole_tile = lax.axis_size("chan") == 2
    step_after = jnp.concatenate([step_size[1:], next_step[None]])
    coef = jnp.concatenate([step_size, factor, step_size * factor - 0.5 * step_after])

    def tiles(block):
        return block.reshape(block.shape[:-1] + (columns, channels))

    def sweep(x, first_row, same, last):
        states, send = drift(x, embed, coef, w_in, w_mid, w_out, first_row, total_rows, same, last)
        earlier_sum, previous = scan_earlier(send[0], None if last else send[1])
        return states, earlier_sum, previous

    def before_of(start, states, earlier_sum, previous):
        level = tiles(start + earlier_sum)
        first = tiles(0.5 * step_size[0] * previous)
        return (level[None] + states).at[0].add(first).astype(jnp.bfloat16)

    if whole_tile:
        swap = [(0, 1), (1, 0)]
        other_guess = lax.ppermute(guess, "chan", swap)
        other_start = lax.ppermute(start_state, "chan", swap)

        def in_order(mine, theirs, axis):
            low = jnp.where(chan == 0, mine, theirs)
            high = jnp.where(chan == 0, theirs, mine)
            return jnp.concatenate([low, high], axis=axis)

        start_full = in_order(start_state, other_start, 0)
        layer_full = tiles(in_order(guess, other_guess, 1))
        for _ in range(ITERS - 1):
            x = jnp.pad(layer_full, ((0, 0), (1, 1), (0, 0), (0, 0)))
            parts = sweep(x, jnp.int32(0), True, False)
            layer_full = before_of(start_full, *parts)
        padded = jnp.pad(layer_full, ((0, 0), (3, 3), (0, 0), (0, 0)))
        rimmed = lax.dynamic_slice_in_dim(padded, chan * tile_rows, tile_rows + 6, axis=1)
    else:
        layer_in = tiles(guess)
        for _ in range(ITERS - 1):
            rimmed = padded_2(layer_in, (("chan", 1),), 3)
            parts = sweep(rimmed, chan * tile_rows - 2, False, False)
            layer_in = before_of(start_state, *parts)
        rimmed = padded_2(layer_in, (("chan", 1),), 3)
    states, earlier_sum, _ = sweep(rimmed, chan * tile_rows - 2, False, True)
    states_after = tiles(start_state + earlier_sum)[None] + states
    return states_after.reshape(guess.shape)


def solution(mesh):
    return jax.shard_map(
        shards,
        mesh=mesh,
        in_specs=(
            P(("parts", "chan"), None),
            P(("parts", "tm", "sub"), "chan", None),
            P(),
            P(),
            P(),
            P(),
            P(),
            P("parts"),
            P("parts"),
        ),
        out_specs=P(("parts", "tm", "sub"), "chan", None),
        check_vma=False,
    )
```

```python
import jax
import jax.numpy as jnp
from jax import lax
from jax.experimental import pallas as pl
from jax.experimental.pallas import tpu as pltpu
from jax.sharding import PartitionSpec as P

ITERS = 2
TIME_AXES = ("tm", "sub")


def padded_2(block, sides, width):
    for axis, dim in sides:
        count = lax.axis_size(axis)
        forward = [(i, i + 1) for i in range(count - 1)]
        backward = [(target, source) for source, target in forward]
        low = lax.ppermute(
            lax.slice_in_dim(block, block.shape[dim] - width, None, axis=dim), axis, forward
        )
        high = lax.ppermute(lax.slice_in_dim(block, 0, width, axis=dim), axis, backward)
        block = jnp.concatenate([low, block, high], axis=dim)
    return block


def conv3x3(src_ref, w_ref, rows_out):
    steps, _, columns, channels_in = src_ref.shape
    channels_out = w_ref.shape[0]
    size = steps * rows_out * columns
    taps = []
    for col_off in range(3):
        acc = None
        for row_off in range(3):
            patch = src_ref[:, row_off : row_off + rows_out].reshape(size, channels_in)
            tap = row_off * 3 + col_off
            weight = w_ref[:, tap * channels_in : (tap + 1) * channels_in]
            part = lax.dot_general(
                patch, weight, (((1,), (1,)), ((), ())), preferred_element_type=jnp.float32
            )
            acc = part if acc is None else acc + part
        taps.append(acc)
    column = lax.broadcasted_iota(jnp.int32, (steps * rows_out, columns, channels_out), 1)
    column = column.reshape(size, channels_out)
    left = jnp.where(column == 0, 0.0, pltpu.roll(taps[0], 1, 0))
    right = jnp.where(column == columns - 1, 0.0, pltpu.roll(taps[2], size - 1, 0))
    return (left + taps[1] + right).reshape(steps, rows_out, columns, channels_out)


def silu(v):
    return v / (1.0 + jnp.exp(-v))


def row_valid(shape, first_row, total_rows):
    rows = first_row + lax.broadcasted_iota(jnp.int32, shape, 1)
    return (rows >= 0) & (rows < total_rows)


def drift_kernel(total_rows, same, last, first_ref, coef_ref, x_ref, emb_ref, w1_ref, w2_ref, w3_ref, states_ref, send_ref, h1_ref, h2_ref):
    first_row = first_ref[0]
    margin = 1 if same else 0
    rows_1 = h1_ref.shape[1] - 2 * margin
    rows_2 = h2_ref.shape[1] - 2 * margin
    steps = x_ref.shape[0]
    act = conv3x3(x_ref, w1_ref, rows_1) + emb_ref[...][:, None, None, :]
    act = jnp.where(row_valid(act.shape, first_row, total_rows), silu(act), 0.0)
    store_hidden(h1_ref, act.astype(jnp.bfloat16), margin)
    act = conv3x3(h1_ref, w2_ref, rows_2)
    act = jnp.where(row_valid(act.shape, first_row + 1 - margin, total_rows), silu(act), 0.0)
    store_hidden(h2_ref, act.astype(jnp.bfloat16), margin)
    drift_now = conv3x3(h2_ref, w3_ref, states_ref.shape[1])
    level = None
    handed_on = None
    for n in range(steps):
        step, factor, weight = coef_ref[n], coef_ref[steps + n], coef_ref[2 * steps + n]
        increment = step * (factor * drift_now[n] - (0.5 * drift_now[n - 1] if n else 0.0))
        if last:
            level = increment if level is None else level + increment
            states_ref[n] = level
        else:
            states_ref[n] = jnp.zeros_like(increment) if level is None else level
            level = increment if level is None else level + increment
        term = weight * drift_now[n]
        handed_on = term if handed_on is None else handed_on + term
    send_ref[0] = handed_on
    if not last:
        send_ref[1] = drift_now[steps - 1]


def store_hidden(ref, value, margin):
    if margin:
        edge = jnp.zeros((ref.shape[0], margin) + ref.shape[2:], ref.dtype)
        ref[:, :margin] = edge
        ref[:, ref.shape[1] - margin :] = edge
        ref[:, margin : ref.shape[1] - margin] = value
    else:
        ref[...] = value


def drift(x, embed, coef, w_in, w_mid, w_out, first_row, total_rows, same, last):
    steps_dev, rows_in, columns, channels = x.shape
    hidden = w_in.shape[1]
    margin = 1 if same else 0
    rows_1 = rows_in - 2
    rows_2 = rows_1 + 2 * margin - 2
    rows_3 = rows_2 + 2 * margin - 2
    w1, w2, w3 = w_in.T, w_mid.T, w_out.T
    flops = 2 * steps_dev * columns * 9 * hidden * (channels * rows_1 + hidden * rows_2 + channels * rows_3)
    vmem = pl.BlockSpec(memory_space=pltpu.VMEM)
    smem = pl.BlockSpec(memory_space=pltpu.SMEM)
    tile = (rows_3, columns, channels)
    states, send = pl.pallas_call(
        lambda *refs: drift_kernel(total_rows, same, last, *refs),
        out_shape=(
            jax.ShapeDtypeStruct((steps_dev,) + tile, jnp.float32),
            jax.ShapeDtypeStruct((1 if last else 2,) + tile, jnp.float32),
        ),
        in_specs=[smem, smem] + [vmem] * 5,
        out_specs=(vmem, vmem),
        scratch_shapes=[
            pltpu.VMEM((steps_dev, rows_1 + 2 * margin, columns, hidden), jnp.bfloat16),
            pltpu.VMEM((steps_dev, rows_2 + 2 * margin, columns, hidden), jnp.bfloat16),
        ],
        compiler_params=pltpu.CompilerParams(vmem_limit_bytes=48 * 1024 * 1024),
        cost_estimate=pl.CostEstimate(
            flops=flops,
            transcendentals=steps_dev * columns * hidden * (rows_1 + rows_2),
            bytes_accessed=2 * (w1.size + w2.size + w3.size) + 2 * x.size + 4 * (steps_dev + 2) * rows_3 * columns * channels,
        ),
    )(jnp.reshape(first_row, (1,)).astype(jnp.int32), coef, x, embed, w1, w2, w3)
    return states, lax.optimization_barrier(send.reshape(send.shape[0], rows_3, columns * channels))


def shifted(array, by):
    devices = lax.axis_size(TIME_AXES)
    pairs = [(i, i + by) for i in range(devices - by)]
    return lax.ppermute(array, TIME_AXES, pairs)


def scan_earlier(total, carried):
    devices = lax.axis_size(TIME_AXES)
    earlier = None
    window = total
    moved = None
    stride = 1
    while stride < devices:
        radix = 2 if stride == 1 else 8
        got_all = []
        for k in range(1, radix):
            by = k * stride
            if by >= devices:
                break
            if by == 1 and carried is not None:
                both = shifted(jnp.stack([window, carried]), 1)
                got, moved = both[0], both[1]
            else:
                got = shifted(window, by)
            got_all.append(got)
        gathered = got_all[0]
        for got in got_all[1:]:
            gathered = gathered + got
        earlier = gathered if earlier is None else earlier + gathered
        stride *= radix
        if stride < devices:
            window = window + gathered
    return earlier, moved


def shards(start_state, guess, w_in, w_mid, w_out, time_embed, levels, plan, offset):
    steps_dev = guess.shape[0]
    devices = lax.axis_size(TIME_AXES)
    time_index = lax.axis_index(TIME_AXES)
    first_step = time_index * steps_dev
    positions = offset[0] + first_step + jnp.arange(steps_dev + 2, dtype=jnp.int32)
    picked = positions[:, None] == jnp.arange(plan.shape[0], dtype=jnp.int32)[None, :]
    all_ids = jnp.sum(jnp.where(picked, plan[None, :], 0), axis=1)
    one_hot = all_ids[:, None] == jnp.arange(levels.shape[0], dtype=jnp.int32)[None, :]
    noise = jnp.dot(one_hot.astype(jnp.float32), levels, precision=lax.Precision.HIGHEST)
    step_size = noise[1 : steps_dev + 1] - noise[:steps_dev]
    next_step = jnp.where(time_index < devices - 1, noise[steps_dev + 1] - noise[steps_dev], 0.0)
    embed = jnp.dot(
        one_hot[:steps_dev].astype(jnp.bfloat16), time_embed, preferred_element_type=jnp.float32
    )
    factor = jnp.where(first_step + jnp.arange(steps_dev, dtype=jnp.int32) == 0, 1.0, 1.5).astype(
        jnp.float32
    )
    channels = w_out.shape[1]
    tile_rows = guess.shape[1]
    columns = guess.shape[2] // channels
    chan = lax.axis_index("chan")
    total_rows = tile_rows * lax.axis_size("chan")
    whole_tile = lax.axis_size("chan") == 2
    step_after = jnp.concatenate([step_size[1:], next_step[None]])
    coef = jnp.concatenate([step_size, factor, step_size * factor - 0.5 * step_after])

    def tiles(block):
        return block.reshape(block.shape[:-1] + (columns, channels))

    def sweep(x, first_row, same, last):
        states, send = drift(x, embed, coef, w_in, w_mid, w_out, first_row, total_rows, same, last)
        earlier_sum, previous = scan_earlier(send[0], None if last else send[1])
        return states, earlier_sum, previous

    def before_of(start, states, earlier_sum, previous):
        level = tiles(start + earlier_sum)
        first = tiles(0.5 * step_size[0] * previous)
        return (level[None] + states).at[0].add(first).astype(jnp.bfloat16)

    if whole_tile:
        swap = [(0, 1), (1, 0)]
        other_guess = lax.ppermute(guess, "chan", swap)
        other_start = lax.ppermute(start_state, "chan", swap)

        def in_order(mine, theirs, axis):
            low = jnp.where(chan == 0, mine, theirs)
            high = jnp.where(chan == 0, theirs, mine)
            return jnp.concatenate([low, high], axis=axis)

        start_full = in_order(start_state, other_start, 0)
        layer_full = tiles(in_order(guess, other_guess, 1))
        for _ in range(ITERS - 1):
            x = jnp.pad(layer_full, ((0, 0), (1, 1), (0, 0), (0, 0)))
            parts = sweep(x, jnp.int32(0), True, False)
            layer_full = before_of(start_full, *parts)
        padded = jnp.pad(layer_full, ((0, 0), (3, 3), (0, 0), (0, 0)))
        rimmed = lax.dynamic_slice_in_dim(padded, chan * tile_rows, tile_rows + 6, axis=1)
    else:
        layer_in = tiles(guess)
        for _ in range(ITERS - 1):
            rimmed = padded_2(layer_in, (("chan", 1),), 3)
            parts = sweep(rimmed, chan * tile_rows - 2, False, False)
            layer_in = before_of(start_state, *parts)
        rimmed = padded_2(layer_in, (("chan", 1),), 3)
    states, earlier_sum, _ = sweep(rimmed, chan * tile_rows - 2, False, True)
    return (start_state + earlier_sum)[None] + states.reshape(guess.shape)


def solution(mesh):
    return jax.shard_map(
        shards,
        mesh=mesh,
        in_specs=(
            P(("parts", "chan"), None),
            P(("parts", "tm", "sub"), "chan", None),
            P(),
            P(),
            P(),
            P(),
            P(),
            P("parts"),
            P("parts"),
        ),
        out_specs=P(("parts", "tm", "sub"), "chan", None),
        check_vma=False,
    )
```

```python
import jax
import jax.numpy as jnp
from jax import lax
from jax.experimental import pallas as pl
from jax.experimental.pallas import tpu as pltpu
from jax.sharding import PartitionSpec as P

ITERS = 2
TIME_AXES = ("tm", "sub")


def padded_2(block, sides, width):
    for axis, dim in sides:
        count = lax.axis_size(axis)
        forward = [(i, i + 1) for i in range(count - 1)]
        backward = [(target, source) for source, target in forward]
        low = lax.ppermute(
            lax.slice_in_dim(block, block.shape[dim] - width, None, axis=dim), axis, forward
        )
        high = lax.ppermute(lax.slice_in_dim(block, 0, width, axis=dim), axis, backward)
        block = jnp.concatenate([low, block, high], axis=dim)
    return block


def conv3x3(src_ref, w_ref, rows_out):
    steps, _, columns, channels_in = src_ref.shape
    channels_out = w_ref.shape[0]
    size = steps * rows_out * columns
    taps = []
    for col_off in range(3):
        acc = None
        for row_off in range(3):
            patch = src_ref[:, row_off : row_off + rows_out].reshape(size, channels_in)
            tap = row_off * 3 + col_off
            weight = w_ref[:, tap * channels_in : (tap + 1) * channels_in]
            part = lax.dot_general(
                patch, weight, (((1,), (1,)), ((), ())), preferred_element_type=jnp.float32
            )
            acc = part if acc is None else acc + part
        taps.append(acc)
    column = lax.broadcasted_iota(jnp.int32, (steps * rows_out, columns, channels_out), 1)
    column = column.reshape(size, channels_out)
    left = jnp.where(column == 0, 0.0, pltpu.roll(taps[0], 1, 0))
    right = jnp.where(column == columns - 1, 0.0, pltpu.roll(taps[2], size - 1, 0))
    return (left + taps[1] + right).reshape(steps, rows_out, columns, channels_out)


def silu(v):
    return v / (1.0 + jnp.exp(-v))


def row_valid(shape, first_row, total_rows):
    rows = first_row + lax.broadcasted_iota(jnp.int32, shape, 1)
    return (rows >= 0) & (rows < total_rows)


def lookups(steps, sc_ref, plan_ref, levels_ref, temb_ref, coef_out, emb_out):
    first_step, final = sc_ref[1], sc_ref[2]
    base = sc_ref[0] + first_step
    top = plan_ref.shape[0] - 1
    ids = [plan_ref[jnp.minimum(base + n, top)] for n in range(steps + 2)]
    noise = [levels_ref[i] for i in ids]
    step = [noise[n + 1] - noise[n] for n in range(steps)]
    after = step[1:] + [jnp.where(final == 0, noise[steps + 1] - noise[steps], 0.0)]
    for n in range(steps):
        factor = jnp.where(first_step + n == 0, 1.0, 1.5).astype(jnp.float32)
        coef_out[n] = step[n]
        coef_out[steps + n] = factor
        coef_out[2 * steps + n] = step[n] * factor - 0.5 * after[n]
    shape = (steps, temb_ref.shape[1])
    row = lax.broadcasted_iota(jnp.int32, shape, 0)
    target = jnp.full(shape, ids[0], jnp.int32)
    for n in range(1, steps):
        target = jnp.where(row == n, ids[n], target)
    one_hot = (lax.broadcasted_iota(jnp.int32, shape, 1) == target).astype(temb_ref.dtype)
    emb_out[...] = lax.dot_general(
        one_hot, temb_ref[...], (((1,), (1,)), ((), ())), preferred_element_type=jnp.float32
    )


def drift_kernel(total_rows, same, last, first, *refs):
    if first:
        (first_ref, sc_ref, plan_ref, levels_ref, temb_ref, x_ref, w1_ref, w2_ref, w3_ref,
         states_ref, send_ref, coef_ref, emb_ref, h1_ref, h2_ref) = refs
        lookups(x_ref.shape[0], sc_ref, plan_ref, levels_ref, temb_ref, coef_ref, emb_ref)
    else:
        (first_ref, coef_ref, emb_ref, x_ref, w1_ref, w2_ref, w3_ref,
         states_ref, send_ref, h1_ref, h2_ref) = refs
    first_row = first_ref[0]
    margin = 1 if same else 0
    rows_1 = h1_ref.shape[1] - 2 * margin
    rows_2 = h2_ref.shape[1] - 2 * margin
    steps = x_ref.shape[0]
    act = conv3x3(x_ref, w1_ref, rows_1) + emb_ref[...][:, None, None, :]
    act = jnp.where(row_valid(act.shape, first_row, total_rows), silu(act), 0.0)
    store_hidden(h1_ref, act.astype(jnp.bfloat16), margin)
    act = conv3x3(h1_ref, w2_ref, rows_2)
    act = jnp.where(row_valid(act.shape, first_row + 1 - margin, total_rows), silu(act), 0.0)
    store_hidden(h2_ref, act.astype(jnp.bfloat16), margin)
    drift_now = conv3x3(h2_ref, w3_ref, states_ref.shape[1])
    level = None
    handed_on = None
    for n in range(steps):
        step, factor, weight = coef_ref[n], coef_ref[steps + n], coef_ref[2 * steps + n]
        increment = step * (factor * drift_now[n] - (0.5 * drift_now[n - 1] if n else 0.0))
        if last:
            level = increment if level is None else level + increment
            states_ref[n] = level
        else:
            states_ref[n] = jnp.zeros_like(increment) if level is None else level
            level = increment if level is None else level + increment
        term = weight * drift_now[n]
        handed_on = term if handed_on is None else handed_on + term
    send_ref[0] = handed_on
    if not last:
        send_ref[1] = drift_now[steps - 1]


def store_hidden(ref, value, margin):
    if margin:
        edge = jnp.zeros((ref.shape[0], margin) + ref.shape[2:], ref.dtype)
        ref[:, :margin] = edge
        ref[:, ref.shape[1] - margin :] = edge
        ref[:, margin : ref.shape[1] - margin] = value
    else:
        ref[...] = value


def drift(x, tables, w_in, w_mid, w_out, first_row, total_rows, same, last):
    first = len(tables) == 4
    steps_dev, rows_in, columns, channels = x.shape
    hidden = w_in.shape[1]
    margin = 1 if same else 0
    rows_1 = rows_in - 2
    rows_2 = rows_1 + 2 * margin - 2
    rows_3 = rows_2 + 2 * margin - 2
    w1, w2, w3 = w_in.T, w_mid.T, w_out.T
    flops = 2 * steps_dev * columns * 9 * hidden * (channels * rows_1 + hidden * rows_2 + channels * rows_3)
    vmem = pl.BlockSpec(memory_space=pltpu.VMEM)
    smem = pl.BlockSpec(memory_space=pltpu.SMEM)
    tile = (rows_3, columns, channels)
    out_shape = [
        jax.ShapeDtypeStruct((steps_dev,) + tile, jnp.float32),
        jax.ShapeDtypeStruct((1 if last else 2,) + tile, jnp.float32),
    ]
    out_specs = [vmem, vmem]
    if first:
        scalars, plan, levels, time_embed = tables
        tables = (scalars, plan, levels, time_embed.T)
        table_specs = [smem, smem, smem, vmem]
        out_shape += [
            jax.ShapeDtypeStruct((3 * steps_dev,), jnp.float32),
            jax.ShapeDtypeStruct((steps_dev, hidden), jnp.float32),
        ]
        out_specs += [smem, vmem]
    else:
        table_specs = [smem, vmem]
    outs = pl.pallas_call(
        lambda *refs: drift_kernel(total_rows, same, last, first, *refs),
        out_shape=tuple(out_shape),
        in_specs=[smem] + table_specs + [vmem] * 4,
        out_specs=tuple(out_specs),
        scratch_shapes=[
            pltpu.VMEM((steps_dev, rows_1 + 2 * margin, columns, hidden), jnp.bfloat16),
            pltpu.VMEM((steps_dev, rows_2 + 2 * margin, columns, hidden), jnp.bfloat16),
        ],
        compiler_params=pltpu.CompilerParams(vmem_limit_bytes=48 * 1024 * 1024),
        cost_estimate=pl.CostEstimate(
            flops=flops,
            transcendentals=steps_dev * columns * hidden * (rows_1 + rows_2),
            bytes_accessed=2 * (w1.size + w2.size + w3.size) + 2 * x.size + 4 * (steps_dev + 2) * rows_3 * columns * channels,
        ),
    )(jnp.reshape(first_row, (1,)).astype(jnp.int32), *tables, x, w1, w2, w3)
    states, send = outs[0], outs[1]
    send = lax.optimization_barrier(send.reshape(send.shape[0], rows_3, columns * channels))
    return states, send, tuple(outs[2:])


def shifted(array, by):
    devices = lax.axis_size(TIME_AXES)
    pairs = [(i, i + by) for i in range(devices - by)]
    return lax.ppermute(array, TIME_AXES, pairs)


def scan_earlier(total, carried):
    devices = lax.axis_size(TIME_AXES)
    earlier = None
    window = total
    moved = None
    stride = 1
    while stride < devices:
        radix = 2 if stride == 1 else 8
        got_all = []
        for k in range(1, radix):
            by = k * stride
            if by >= devices:
                break
            if by == 1 and carried is not None:
                both = shifted(jnp.stack([window, carried]), 1)
                got, moved = both[0], both[1]
            else:
                got = shifted(window, by)
            got_all.append(got)
        gathered = got_all[0]
        for got in got_all[1:]:
            gathered = gathered + got
        earlier = gathered if earlier is None else earlier + gathered
        stride *= radix
        if stride < devices:
            window = window + gathered
    return earlier, moved


def shards(start_state, guess, w_in, w_mid, w_out, time_embed, levels, plan, offset):
    steps_dev = guess.shape[0]
    devices = lax.axis_size(TIME_AXES)
    time_index = lax.axis_index(TIME_AXES)
    first_step = time_index * steps_dev
    final = (time_index == devices - 1).astype(jnp.int32)
    tables = (jnp.stack([offset[0], first_step, final]).astype(jnp.int32), plan, levels, time_embed)
    step_first = []
    channels = w_out.shape[1]
    tile_rows = guess.shape[1]
    columns = guess.shape[2] // channels
    chan = lax.axis_index("chan")
    total_rows = tile_rows * lax.axis_size("chan")
    whole_tile = lax.axis_size("chan") == 2

    def tiles(block):
        return block.reshape(block.shape[:-1] + (columns, channels))

    def sweep(x, first_row, same, last):
        nonlocal tables
        states, send, found = drift(x, tables, w_in, w_mid, w_out, first_row, total_rows, same, last)
        if found:
            tables = found
            step_first.append(found[0][0])
        earlier_sum, previous = scan_earlier(send[0], None if last else send[1])
        return states, earlier_sum, previous

    def before_of(start, states, earlier_sum, previous):
        level = tiles(start + earlier_sum)
        first = tiles(0.5 * step_first[0] * previous)
        return (level[None] + states).at[0].add(first).astype(jnp.bfloat16)

    if whole_tile:
        swap = [(0, 1), (1, 0)]
        other_guess = lax.ppermute(guess, "chan", swap)
        other_start = lax.ppermute(start_state, "chan", swap)

        def in_order(mine, theirs, axis):
            low = jnp.where(chan == 0, mine, theirs)
            high = jnp.where(chan == 0, theirs, mine)
            return jnp.concatenate([low, high], axis=axis)

        start_full = in_order(start_state, other_start, 0)
        layer_full = tiles(in_order(guess, other_guess, 1))
        for _ in range(ITERS - 1):
            x = jnp.pad(layer_full, ((0, 0), (1, 1), (0, 0), (0, 0)))
            parts = sweep(x, jnp.int32(0), True, False)
            layer_full = before_of(start_full, *parts)
        padded = jnp.pad(layer_full, ((0, 0), (3, 3), (0, 0), (0, 0)))
        rimmed = lax.dynamic_slice_in_dim(padded, chan * tile_rows, tile_rows + 6, axis=1)
    else:
        layer_in = tiles(guess)
        for _ in range(ITERS - 1):
            rimmed = padded_2(layer_in, (("chan", 1),), 3)
            parts = sweep(rimmed, chan * tile_rows - 2, False, False)
            layer_in = before_of(start_state, *parts)
        rimmed = padded_2(layer_in, (("chan", 1),), 3)
    states, earlier_sum, _ = sweep(rimmed, chan * tile_rows - 2, False, True)
    return (start_state + earlier_sum)[None] + states.reshape(guess.shape)


def solution(mesh):
    return jax.shard_map(
        shards,
        mesh=mesh,
        in_specs=(
            P(("parts", "chan"), None),
            P(("parts", "tm", "sub"), "chan", None),
            P(),
            P(),
            P(),
            P(),
            P(),
            P("parts"),
            P("parts"),
        ),
        out_specs=P(("parts", "tm", "sub"), "chan", None),
        check_vma=False,
    )
```

```python
import jax
import jax.numpy as jnp
from jax import lax
from jax.experimental import pallas as pl
from jax.experimental.pallas import tpu as pltpu
from jax.sharding import PartitionSpec as P

ITERS = 2
TIME_AXES = ("tm", "sub")


def padded_2(block, sides, width):
    for axis, dim in sides:
        count = lax.axis_size(axis)
        forward = [(i, i + 1) for i in range(count - 1)]
        backward = [(target, source) for source, target in forward]
        low = lax.ppermute(
            lax.slice_in_dim(block, block.shape[dim] - width, None, axis=dim), axis, forward
        )
        high = lax.ppermute(lax.slice_in_dim(block, 0, width, axis=dim), axis, backward)
        block = jnp.concatenate([low, block, high], axis=dim)
    return block


def conv3x3(src_ref, w_ref, rows_out):
    steps, _, columns, channels_in = src_ref.shape
    channels_out = w_ref.shape[0]
    size = steps * rows_out * columns
    taps = []
    for col_off in range(3):
        acc = None
        for row_off in range(3):
            patch = src_ref[:, row_off : row_off + rows_out].reshape(size, channels_in)
            tap = row_off * 3 + col_off
            weight = w_ref[:, tap * channels_in : (tap + 1) * channels_in]
            part = lax.dot_general(
                patch, weight, (((1,), (1,)), ((), ())), preferred_element_type=jnp.float32
            )
            acc = part if acc is None else acc + part
        taps.append(acc)
    column = lax.broadcasted_iota(jnp.int32, (steps * rows_out, columns, channels_out), 1)
    column = column.reshape(size, channels_out)
    left = jnp.where(column == 0, 0.0, pltpu.roll(taps[0], 1, 0))
    right = jnp.where(column == columns - 1, 0.0, pltpu.roll(taps[2], size - 1, 0))
    return (left + taps[1] + right).reshape(steps, rows_out, columns, channels_out)


def silu(v):
    return v * (0.5 + 0.5 * jnp.tanh(0.5 * v))


def row_valid(shape, first_row, total_rows):
    rows = first_row + lax.broadcasted_iota(jnp.int32, shape, 1)
    return (rows >= 0) & (rows < total_rows)


def drift_kernel(total_rows, same, last, first_ref, coef_ref, x_ref, emb_ref, w1_ref, w2_ref, w3_ref, states_ref, send_ref, h1_ref, h2_ref):
    first_row = first_ref[0]
    margin = 1 if same else 0
    rows_1 = h1_ref.shape[1] - 2 * margin
    rows_2 = h2_ref.shape[1] - 2 * margin
    steps = x_ref.shape[0]
    act = conv3x3(x_ref, w1_ref, rows_1) + emb_ref[...][:, None, None, :]
    act = jnp.where(row_valid(act.shape, first_row, total_rows), silu(act), 0.0)
    store_hidden(h1_ref, act.astype(jnp.bfloat16), margin)
    act = conv3x3(h1_ref, w2_ref, rows_2)
    act = jnp.where(row_valid(act.shape, first_row + 1 - margin, total_rows), silu(act), 0.0)
    store_hidden(h2_ref, act.astype(jnp.bfloat16), margin)
    drift_now = conv3x3(h2_ref, w3_ref, states_ref.shape[1])
    level = None
    handed_on = None
    for n in range(steps):
        step, factor, weight = coef_ref[n], coef_ref[steps + n], coef_ref[2 * steps + n]
        increment = step * (factor * drift_now[n] - (0.5 * drift_now[n - 1] if n else 0.0))
        if last:
            level = increment if level is None else level + increment
            states_ref[n] = level
        else:
            states_ref[n] = jnp.zeros_like(increment) if level is None else level
            level = increment if level is None else level + increment
        term = weight * drift_now[n]
        handed_on = term if handed_on is None else handed_on + term
    send_ref[0] = handed_on
    if not last:
        send_ref[1] = drift_now[steps - 1]


def store_hidden(ref, value, margin):
    if margin:
        edge = jnp.zeros((ref.shape[0], margin) + ref.shape[2:], ref.dtype)
        ref[:, :margin] = edge
        ref[:, ref.shape[1] - margin :] = edge
        ref[:, margin : ref.shape[1] - margin] = value
    else:
        ref[...] = value


def drift(x, embed, coef, w_in, w_mid, w_out, first_row, total_rows, same, last):
    steps_dev, rows_in, columns, channels = x.shape
    hidden = w_in.shape[1]
    margin = 1 if same else 0
    rows_1 = rows_in - 2
    rows_2 = rows_1 + 2 * margin - 2
    rows_3 = rows_2 + 2 * margin - 2
    w1, w2, w3 = w_in.T, w_mid.T, w_out.T
    flops = 2 * steps_dev * columns * 9 * hidden * (channels * rows_1 + hidden * rows_2 + channels * rows_3)
    vmem = pl.BlockSpec(memory_space=pltpu.VMEM)
    smem = pl.BlockSpec(memory_space=pltpu.SMEM)
    tile = (rows_3, columns, channels)
    states, send = pl.pallas_call(
        lambda *refs: drift_kernel(total_rows, same, last, *refs),
        out_shape=(
            jax.ShapeDtypeStruct((steps_dev,) + tile, jnp.float32),
            jax.ShapeDtypeStruct((1 if last else 2,) + tile, jnp.float32),
        ),
        in_specs=[smem, smem] + [vmem] * 5,
        out_specs=(vmem, vmem),
        scratch_shapes=[
            pltpu.VMEM((steps_dev, rows_1 + 2 * margin, columns, hidden), jnp.bfloat16),
            pltpu.VMEM((steps_dev, rows_2 + 2 * margin, columns, hidden), jnp.bfloat16),
        ],
        compiler_params=pltpu.CompilerParams(vmem_limit_bytes=48 * 1024 * 1024),
        cost_estimate=pl.CostEstimate(
            flops=flops,
            transcendentals=steps_dev * columns * hidden * (rows_1 + rows_2),
            bytes_accessed=2 * (w1.size + w2.size + w3.size) + 2 * x.size + 4 * (steps_dev + 2) * rows_3 * columns * channels,
        ),
    )(jnp.reshape(first_row, (1,)).astype(jnp.int32), coef, x, embed, w1, w2, w3)
    return states, lax.optimization_barrier(send.reshape(send.shape[0], rows_3, columns * channels))


def shifted(array, by):
    devices = lax.axis_size(TIME_AXES)
    pairs = [(i, i + by) for i in range(devices - by)]
    return lax.ppermute(array, TIME_AXES, pairs)


def scan_earlier(total, carried):
    devices = lax.axis_size(TIME_AXES)
    earlier = None
    window = total
    moved = None
    stride = 1
    while stride < devices:
        radix = 2 if stride == 1 else 8
        got_all = []
        for k in range(1, radix):
            by = k * stride
            if by >= devices:
                break
            if by == 1 and carried is not None:
                both = shifted(jnp.stack([window, carried]), 1)
                got, moved = both[0], both[1]
            else:
                got = shifted(window, by)
            got_all.append(got)
        gathered = got_all[0]
        for got in got_all[1:]:
            gathered = gathered + got
        earlier = gathered if earlier is None else earlier + gathered
        stride *= radix
        if stride < devices:
            window = window + gathered
    return earlier, moved


def shards(start_state, guess, w_in, w_mid, w_out, time_embed, levels, plan, offset):
    steps_dev = guess.shape[0]
    devices = lax.axis_size(TIME_AXES)
    time_index = lax.axis_index(TIME_AXES)
    first_step = time_index * steps_dev
    positions = offset[0] + first_step + jnp.arange(steps_dev + 2, dtype=jnp.int32)
    picked = positions[:, None] == jnp.arange(plan.shape[0], dtype=jnp.int32)[None, :]
    all_ids = jnp.sum(jnp.where(picked, plan[None, :], 0), axis=1)
    one_hot = all_ids[:, None] == jnp.arange(levels.shape[0], dtype=jnp.int32)[None, :]
    noise = jnp.dot(one_hot.astype(jnp.float32), levels, precision=lax.Precision.HIGHEST)
    step_size = noise[1 : steps_dev + 1] - noise[:steps_dev]
    next_step = jnp.where(time_index < devices - 1, noise[steps_dev + 1] - noise[steps_dev], 0.0)
    embed = jnp.dot(
        one_hot[:steps_dev].astype(jnp.bfloat16), time_embed, preferred_element_type=jnp.float32
    )
    factor = jnp.where(first_step + jnp.arange(steps_dev, dtype=jnp.int32) == 0, 1.0, 1.5).astype(
        jnp.float32
    )
    channels = w_out.shape[1]
    tile_rows = guess.shape[1]
    columns = guess.shape[2] // channels
    chan = lax.axis_index("chan")
    total_rows = tile_rows * lax.axis_size("chan")
    whole_tile = lax.axis_size("chan") == 2
    step_after = jnp.concatenate([step_size[1:], next_step[None]])
    coef = jnp.concatenate([step_size, factor, step_size * factor - 0.5 * step_after])

    def tiles(block):
        return block.reshape(block.shape[:-1] + (columns, channels))

    def sweep(x, first_row, same, last):
        states, send = drift(x, embed, coef, w_in, w_mid, w_out, first_row, total_rows, same, last)
        earlier_sum, previous = scan_earlier(send[0], None if last else send[1])
        return states, earlier_sum, previous

    def before_of(start, states, earlier_sum, previous):
        level = tiles(start + earlier_sum)
        first = tiles(0.5 * step_size[0] * previous)
        return (level[None] + states).at[0].add(first).astype(jnp.bfloat16)

    if whole_tile:
        swap = [(0, 1), (1, 0)]
        other_guess = lax.ppermute(guess, "chan", swap)
        other_start = lax.ppermute(start_state, "chan", swap)

        def in_order(mine, theirs, axis):
            low = jnp.where(chan == 0, mine, theirs)
            high = jnp.where(chan == 0, theirs, mine)
            return jnp.concatenate([low, high], axis=axis)

        start_full = in_order(start_state, other_start, 0)
        layer_full = tiles(in_order(guess, other_guess, 1))
        for _ in range(ITERS - 1):
            x = jnp.pad(layer_full, ((0, 0), (1, 1), (0, 0), (0, 0)))
            parts = sweep(x, jnp.int32(0), True, False)
            layer_full = before_of(start_full, *parts)
        padded = jnp.pad(layer_full, ((0, 0), (3, 3), (0, 0), (0, 0)))
        rimmed = lax.dynamic_slice_in_dim(padded, chan * tile_rows, tile_rows + 6, axis=1)
    else:
        layer_in = tiles(guess)
        for _ in range(ITERS - 1):
            rimmed = padded_2(layer_in, (("chan", 1),), 3)
            parts = sweep(rimmed, chan * tile_rows - 2, False, False)
            layer_in = before_of(start_state, *parts)
        rimmed = padded_2(layer_in, (("chan", 1),), 3)
    states, earlier_sum, _ = sweep(rimmed, chan * tile_rows - 2, False, True)
    return (start_state + earlier_sum)[None] + states.reshape(guess.shape)


def solution(mesh):
    return jax.shard_map(
        shards,
        mesh=mesh,
        in_specs=(
            P(("parts", "chan"), None),
            P(("parts", "tm", "sub"), "chan", None),
            P(),
            P(),
            P(),
            P(),
            P(),
            P("parts"),
            P("parts"),
        ),
        out_specs=P(("parts", "tm", "sub"), "chan", None),
        check_vma=False,
    )
```
